1024 devices in a mesh: ctx: 64 (over z_lo, y, core), head: 16 (over x, z_hi).
Axes of the slice: x: 4, y: 4, z: 32 (z_hi: 4, z_lo: 8; z = z_hi * 8 + z_lo), core: 2. Of those that a mesh axis runs over, the one named last changes fastest.
Arguments:
- query_matrix: bfloat16 [32768, 4096], P(('ctx', 'head')), may hold values from -40 to 40
- key_matrix: bfloat16 [32768, 2048], P(('ctx', 'head')), may hold values from -40 to 40
- value_matrix: bfloat16 [32768, 2048], P(('ctx', 'head')), may hold values from -6 to 6
- output_gradient: bfloat16 [32768, 4096], P(('ctx', 'head')), may hold values from -6 to 6
- query_gain: float32 [128], replicated, may hold values from 1 to 3.5
- key_gain: float32 [128], replicated, may hold values from 1 to 3.5
- doc_ids: int32 [32768], replicated, may hold values from 0 to 63, never falling along the last dimension, each value on 1 to 1024 neighbouring positions
Outputs:
- attended: bfloat16 [32768, 4096], P(('ctx', 'head'))
- query_gradient: bfloat16 [32768, 4096], P(('ctx', 'head'))
- key_gradient: bfloat16 [32768, 2048], P(('ctx', 'head'))
- value_gradient: bfloat16 [32768, 2048], P(('ctx', 'head'))
The draws below stay inside these ranges and needn't reach their ends.
Inputs may be any that keep to these rules, and one draw needn't show every extreme that they name: `doc_ids`: document ids never fall along the sequence; each document holds 1 to 1024 tokens, and one holds exactly 1024.
All inputs are finite; a program needn't handle non-finite values.
Results may differ from the reference program's by a relative error of at most 0.019.
Values may be sent and summed in bfloat16 or wider, within the bound.
No kernel may reach another device: no remote copies, remote signals or barrier semaphores. Data moves between devices by JAX's collectives and lax.ppermute only.
A program may use at most 32 MiB of HBM per device.

```python
import math
import jax
import jax.numpy as jnp
import numpy as np
from jax import lax

QUERY_HEADS = 32
KEY_VALUE_HEADS = 16
HEAD_WIDTH = 128
TOK_DEV = 512
MAXDOC = 1024
PACKED_TOKENS = 32768
REACH = 2
DOCS = 64


def rescaled_rows(seed_key, row_count, head_count):
    key_base, key_scale = jax.random.split(seed_key, 2)
    row_scale = jnp.exp(jax.random.uniform(key_scale, (row_count, head_count, 1), jnp.float32, 0.0, math.log(10.0)))
    base_draw = jnp.clip(jax.random.normal(key_base, (row_count, head_count, HEAD_WIDTH), jnp.float32), -4.0, 4.0)
    entries = row_scale * base_draw
    return entries.reshape(row_count, head_count * HEAD_WIDTH)


def draw_query_matrix(key, part):
    return rescaled_rows(jax.random.fold_in(key, 11), PACKED_TOKENS, QUERY_HEADS).astype(jnp.bfloat16)


def draw_key_matrix(key, part):
    return rescaled_rows(jax.random.fold_in(key, 23), PACKED_TOKENS, KEY_VALUE_HEADS).astype(jnp.bfloat16)


def block_levels(stream_key, extent, pieces, smallest, largest):
    gain = 1.0
    for position, blocks in pieces:
        steps = jax.random.uniform(jax.random.fold_in(jax.random.fold_in(stream_key, 6), position), (blocks,), jnp.float32, smallest / len(pieces), largest / len(pieces))
        gain = gain * jnp.repeat(jnp.exp(steps), extent[position] // blocks).reshape((-1,) + (1,) * (len(extent) - 1 - position))
    return gain


def length_profile(amount, total, bound, skew):
    weights = [(1 << 20) // math.isqrt(rank ** skew) + 1 for rank in range(2, amount + 1)]
    surplus, given = total - bound - (amount - 1), [1] * (amount - 1)
    while surplus > 0:
        candidates = [i for i in range(amount - 1) if given[i] < bound]
        whole, left = sum([weights[i] for i in candidates]), surplus
        for i in candidates:
            extra = min(bound - given[i], max(1, left * weights[i] // whole), surplus)
            given[i] = given[i] + extra
            surplus = surplus - extra
    return np.array([bound] + given)


def ragged(rng, number_of, total, most, lean):
    if number_of == 2:
        one = jax.random.randint(rng, (), max(1, total - most), min(most, total - 1) + 1)
        return jnp.stack([one, total - one])
    lengths = jnp.asarray(length_profile(number_of, total, most, lean), jnp.int32)
    twos = (number_of - 1) // 2
    source_of, sink = lengths[1:1 + 2 * twos:2], lengths[2:2 + 2 * twos:2]
    margin = jnp.minimum(source_of - 1, most - sink)
    moved = jax.random.randint(jax.random.fold_in(rng, 1), (twos,), 0, 1 << 20) % (margin + 1)
    lengths = lengths.at[1:1 + 2 * twos:2].set(source_of - moved).at[2:2 + 2 * twos:2].set(sink + moved)
    return lengths[jax.random.permutation(jax.random.fold_in(rng, 2), number_of)]


def normal_values(own_key, dims, scale, reach, cuts=(), held_as=jnp.bfloat16):
    values = jax.random.normal(own_key, dims, jnp.float32) * scale
    if len(cuts) > 0:
        values = block_levels(own_key, dims, cuts, -0.22, 0.18) * values
    return jnp.clip(values, min=-reach, max=reach).astype(held_as)


def setup_inputs(seed: int = 0) -> dict:
    streams_of = jax.random.split(jax.random.key(seed), 8)
    query_matrix = draw_query_matrix(jax.random.fold_in(streams_of[7], 71), 0)
    key_matrix = draw_key_matrix(jax.random.fold_in(streams_of[7], 71), 0)
    value_matrix = normal_values(streams_of[2], (PACKED_TOKENS, KEY_VALUE_HEADS * HEAD_WIDTH), 1.0, 6.0, ((0, 1024),))
    output_gradient = normal_values(streams_of[3], (PACKED_TOKENS, QUERY_HEADS * HEAD_WIDTH), 1.0, 6.0, ((0, 1024),))
    query_gain = jnp.clip(jnp.exp(jax.random.uniform(streams_of[4], (HEAD_WIDTH,), jnp.float32, math.log(1.0), math.log(3.5))), 1.0, 3.5)
    key_gain = jnp.clip(jnp.exp(jax.random.uniform(streams_of[5], (HEAD_WIDTH,), jnp.float32, math.log(1.0), math.log(3.5))), 1.0, 3.5)
    doc_ids = jnp.searchsorted(jnp.cumsum(ragged(streams_of[6], DOCS, PACKED_TOKENS, MAXDOC, 2)), jnp.arange(PACKED_TOKENS), side="right").astype(jnp.int32)
    return {"query_matrix": query_matrix, "key_matrix": key_matrix, "value_matrix": value_matrix, "output_gradient": output_gradient, "query_gain": query_gain, "key_gain": key_gain, "doc_ids": doc_ids}


CAP_VALUE = 50.0
QUERY_SCALE = 144.0 ** (-0.5)
EPSILON = 1e-06

def normalize(value_entries, gain_vector, factor):
    inverse = lax.rsqrt(lax.optimization_barrier(jnp.mean(value_entries * value_entries, axis=-1, keepdims=True)) + EPSILON)
    rounded = lax.optimization_barrier((value_entries * inverse * gain_vector * factor).astype(jnp.bfloat16))
    return (inverse, rounded)

def norm_grad(value_entries, inverse, gain_vector, factor, upstream):
    scaled = upstream * gain_vector * factor
    inner_mean = lax.optimization_barrier(jnp.mean(scaled * value_entries, axis=-1, keepdims=True))
    return inverse * (scaled - value_entries * inverse * inverse * inner_mean)

def capped(query_block, key_block, query_docs, key_docs, query_pos, key_pos):
    raw_scores = jnp.einsum('qhge,khe->hgqk', query_block.astype(jnp.float32), key_block.astype(jnp.float32))
    scores = CAP_VALUE * jnp.tanh(raw_scores / CAP_VALUE)
    allowed = (query_docs[:, None] == key_docs[None, :]) & (key_pos[None, :] <= query_pos[:, None])
    return (scores, allowed)

def reference(query_matrix, key_matrix, value_matrix, output_gradient, query_gain, key_gain, doc_ids):
    group_width = QUERY_HEADS // KEY_VALUE_HEADS
    cushion = REACH * TOK_DEV
    window_rows = (REACH + 1) * TOK_DEV
    block_count = PACKED_TOKENS // TOK_DEV
    query_entries = query_matrix.astype(jnp.float32).reshape(PACKED_TOKENS, KEY_VALUE_HEADS, group_width, HEAD_WIDTH)
    key_entries = key_matrix.astype(jnp.float32).reshape(PACKED_TOKENS, KEY_VALUE_HEADS, HEAD_WIDTH)
    query_inv, query_norm = normalize(query_entries, query_gain, QUERY_SCALE)
    key_inv, key_norm_factor = normalize(key_entries, key_gain, 1.0)
    value_entries = value_matrix.reshape(PACKED_TOKENS, KEY_VALUE_HEADS, HEAD_WIDTH)
    gradient_rows = output_gradient.reshape(PACKED_TOKENS, KEY_VALUE_HEADS, group_width, HEAD_WIDTH)
    doc_list = doc_ids.astype(jnp.int32)
    key_padding = jnp.concatenate([jnp.zeros((cushion, KEY_VALUE_HEADS, HEAD_WIDTH), jnp.bfloat16), key_norm_factor], axis=0)
    value_padding = jnp.concatenate([jnp.zeros((cushion, KEY_VALUE_HEADS, HEAD_WIDTH), jnp.bfloat16), value_entries], axis=0)
    doc_pad = jnp.concatenate([jnp.full((cushion,), -1, jnp.int32), doc_list], axis=0)

    def window(block_index):
        row_start = (block_index * TOK_DEV).astype(jnp.int32)
        query_block = lax.dynamic_slice_in_dim(query_norm, row_start, TOK_DEV, 0)
        key_block = lax.dynamic_slice_in_dim(key_padding, row_start, window_rows, 0)
        value_block = lax.dynamic_slice_in_dim(value_padding, row_start, window_rows, 0)
        query_docs = lax.dynamic_slice_in_dim(doc_list, row_start, TOK_DEV, 0)
        key_docs = lax.dynamic_slice_in_dim(doc_pad, row_start, window_rows, 0)
        query_pos = row_start + jnp.arange(TOK_DEV, dtype=jnp.int32)
        key_pos = row_start - cushion + jnp.arange(window_rows, dtype=jnp.int32)
        scores, allowed = capped(query_block, key_block, query_docs, key_docs, query_pos, key_pos)
        return (row_start, query_block, key_block, value_block, scores, allowed)

    def forward(block_index):
        row_start, query_block, key_block, value_block, scores, allowed = window(block_index)
        weights = jnp.where(allowed, jnp.exp(scores), 0.0)
        weight_sum = lax.optimization_barrier(jnp.sum(weights, axis=-1))
        weight_low = lax.optimization_barrier(weights.astype(jnp.bfloat16)).astype(jnp.float32)
        mixed_part = jnp.einsum('hgqk,khe->qhge', weight_low, value_block.astype(jnp.float32))
        attended_block = (mixed_part / jnp.transpose(weight_sum, (2, 0, 1))[..., None]).astype(jnp.bfloat16)
        return (attended_block, jnp.log(weight_sum))
    block_ids = jnp.arange(block_count, dtype=jnp.int32)
    visited_blocks, log_blocks = lax.map(forward, block_ids)
    attended = visited_blocks.reshape(PACKED_TOKENS, KEY_VALUE_HEADS, group_width, HEAD_WIDTH)
    row_inner = lax.optimization_barrier(jnp.sum(gradient_rows.astype(jnp.float32) * attended.astype(jnp.float32), axis=-1))

    def backward(carry, block_index):
        key_acc, value_acc = carry
        row_start, query_block, key_block, value_block, scores, allowed = window(block_index)
        log_total = lax.dynamic_index_in_dim(log_blocks, block_index, 0, keepdims=False)
        prob_block = jnp.where(allowed, jnp.exp(scores - log_total[..., None]), 0.0)
        grad_block = lax.dynamic_slice_in_dim(gradient_rows, row_start, TOK_DEV, 0).astype(jnp.float32)
        inner_block = jnp.transpose(lax.dynamic_slice_in_dim(row_inner, row_start, TOK_DEV, 0), (1, 2, 0))
        dprob = jnp.einsum('qhge,khe->hgqk', grad_block, value_block.astype(jnp.float32))
        dscore = prob_block * (dprob - inner_block[..., None]) * (1.0 - (scores / CAP_VALUE) ** 2)
        dscore_low = lax.optimization_barrier(dscore.astype(jnp.bfloat16)).astype(jnp.float32)
        prob_low = lax.optimization_barrier(prob_block.astype(jnp.bfloat16)).astype(jnp.float32)
        query_part = jnp.einsum('hgqk,khe->qhge', dscore_low, key_block.astype(jnp.float32))
        key_part = jnp.einsum('hgqk,qhge->khe', dscore_low, query_block.astype(jnp.float32))
        value_part = jnp.einsum('hgqk,qhge->khe', prob_low, grad_block)
        key_acc = lax.dynamic_update_slice_in_dim(key_acc, lax.dynamic_slice_in_dim(key_acc, row_start, window_rows, 0) + key_part, row_start, 0)
        value_acc = lax.dynamic_update_slice_in_dim(value_acc, lax.dynamic_slice_in_dim(value_acc, row_start, window_rows, 0) + value_part, row_start, 0)
        return ((key_acc, value_acc), query_part)
    blank_block = jnp.zeros((PACKED_TOKENS + cushion, KEY_VALUE_HEADS, HEAD_WIDTH), jnp.float32)
    (key_acc, value_acc), query_pieces = lax.scan(backward, (blank_block, blank_block), block_ids)
    query_total_sum = query_pieces.reshape(PACKED_TOKENS, KEY_VALUE_HEADS, group_width, HEAD_WIDTH)
    query_gradient = norm_grad(query_entries, query_inv, query_gain, QUERY_SCALE, query_total_sum).astype(jnp.bfloat16)
    key_gradient = norm_grad(key_entries, key_inv, key_gain, 1.0, key_acc[cushion:]).astype(jnp.bfloat16)
    value_gradient = value_acc[cushion:].astype(jnp.bfloat16)
    return (attended.reshape(PACKED_TOKENS, QUERY_HEADS * HEAD_WIDTH), query_gradient.reshape(PACKED_TOKENS, QUERY_HEADS * HEAD_WIDTH), key_gradient.reshape(PACKED_TOKENS, KEY_VALUE_HEADS * HEAD_WIDTH), value_gradient.reshape(PACKED_TOKENS, KEY_VALUE_HEADS * HEAD_WIDTH))
```

```python
import jax
import jax.numpy as jnp
from jax import lax
from jax.sharding import PartitionSpec as P

HEAD_WIDTH = 128
REACH = 2


CAP_VALUE = 50.0
QUERY_SCALE = 144.0 ** (-0.5)
EPSILON = 1e-06


def passed_along(block, axis, distance):
    devices = range(lax.axis_size(axis))
    route = [(i - distance, i) for i in devices if i - distance in devices]
    return lax.ppermute(block, axis, route)


def for_sending(value):

    def short(part):
        return part.astype(jnp.bfloat16) if part.dtype == jnp.float32 else part

    return jax.tree.map(short, value)


def normalize(value_entries, gain_vector, factor):
    inverse = lax.rsqrt(jnp.mean(value_entries * value_entries, axis=-1, keepdims=True) + EPSILON)
    return (inverse, (value_entries * inverse * gain_vector * factor).astype(jnp.bfloat16))


def norm_grad(value_entries, inverse, gain_vector, factor, upstream):
    scaled = upstream * gain_vector * factor
    inner_mean = jnp.mean(scaled * value_entries, axis=-1, keepdims=True)
    return inverse * (scaled - value_entries * inverse * inverse * inner_mean)


def capped(query_block, key_block, query_docs, key_docs, query_pos, key_pos):
    raw_scores = jnp.einsum(
        "qhge,khe->hgqk", query_block, key_block, preferred_element_type=jnp.float32
    )
    scores = CAP_VALUE * jnp.tanh(raw_scores / CAP_VALUE)
    allowed = (query_docs[:, None] == key_docs[None, :]) & (key_pos[None, :] <= query_pos[:, None])
    return (scores, allowed)


def on_device(
    query_matrix, key_matrix, value_matrix, output_gradient, query_gain, key_gain, doc_ids
):
    token_rows, head_devices = query_matrix.shape[0], lax.axis_size("head")
    packed = jnp.concatenate(
        [
            part.reshape(token_rows, head_devices, -1)
            for part in (query_matrix, key_matrix, value_matrix, output_gradient)
        ],
        axis=-1,
    )
    arrived = lax.all_to_all(packed, "head", split_axis=1, concat_axis=0, tiled=True)
    arrived = arrived.reshape(token_rows * head_devices, -1)
    widths = [query_matrix.shape[1] // head_devices, key_matrix.shape[1] // head_devices]
    cuts = [widths[0], widths[0] + widths[1], widths[0] + 2 * widths[1]]
    query_loc = arrived[:, : cuts[0]]
    key_loc = arrived[:, cuts[0] : cuts[1]]
    value_loc = arrived[:, cuts[1] : cuts[2]]
    grad_loc = arrived[:, cuts[2] :]
    row_count = query_loc.shape[0]
    kv_heads = key_loc.shape[1] // HEAD_WIDTH
    group_width = query_loc.shape[1] // key_loc.shape[1]
    query_entries = query_loc.astype(jnp.float32).reshape(
        row_count, kv_heads, group_width, HEAD_WIDTH
    )
    key_entries = key_loc.astype(jnp.float32).reshape(row_count, kv_heads, HEAD_WIDTH)
    query_inv, query_norm = normalize(query_entries, query_gain, QUERY_SCALE)
    key_inv, key_norm_factor = normalize(key_entries, key_gain, 1.0)
    value_entries = value_loc.reshape(row_count, kv_heads, HEAD_WIDTH)
    gradient_rows = grad_loc.reshape(row_count, kv_heads, group_width, HEAD_WIDTH)
    ctx_place = lax.axis_index("ctx")
    row_start = ctx_place * row_count
    query_docs = lax.dynamic_slice_in_dim(doc_ids, row_start, row_count, 0)
    query_pos = row_start + jnp.arange(row_count, dtype=jnp.int32)
    first_doc = query_docs[0]
    remote = [
        passed_along((key_norm_factor, value_entries), "ctx", offset)
        for offset in range(1, REACH + 1)
    ]
    sources = [(key_norm_factor, value_entries)] + remote
    block_infos = []
    for offset in range(REACH + 1):
        owner = ctx_place - offset
        key_docs = lax.dynamic_slice_in_dim(
            doc_ids, jnp.maximum(owner, 0) * row_count, row_count, 0
        )
        key_pos = owner * row_count + jnp.arange(row_count, dtype=jnp.int32)
        needed = (owner >= 0) & ((key_docs[row_count - 1] == first_doc) | (offset == 0))
        block_infos.append((key_docs, key_pos, needed))
    mixed_sum = jnp.zeros((row_count, kv_heads, group_width, HEAD_WIDTH), jnp.float32)
    weight_sum = jnp.zeros((kv_heads, group_width, row_count), jnp.float32)
    for offset in range(REACH + 1):
        key_block, value_block = sources[offset]
        key_docs, key_pos, needed = block_infos[offset]

        def attend(running):
            scores, allowed = capped(
                query_norm, key_block, query_docs, key_docs, query_pos, key_pos
            )
            weights = jnp.where(allowed, jnp.exp(scores), 0.0)
            mixed_part = jnp.einsum(
                "hgqk,khe->qhge",
                weights.astype(jnp.bfloat16),
                value_block,
                preferred_element_type=jnp.float32,
            )
            return (running[0] + mixed_part, running[1] + jnp.sum(weights, axis=-1))

        mixed_sum, weight_sum = lax.cond(
            needed, attend, lambda running: running, (mixed_sum, weight_sum)
        )
    attended = (mixed_sum / jnp.transpose(weight_sum, (2, 0, 1))[..., None]).astype(jnp.bfloat16)
    log_total = jnp.log(weight_sum)
    row_inner = jnp.transpose(
        jnp.sum(gradient_rows.astype(jnp.float32) * attended.astype(jnp.float32), axis=-1),
        (1, 2, 0),
    )
    query_total_sum = jnp.zeros((row_count, kv_heads, group_width, HEAD_WIDTH), jnp.float32)
    partials = []
    for offset in range(REACH + 1):
        key_block, value_block = sources[offset]
        key_docs, key_pos, needed = block_infos[offset]

        def differentiate():
            scores, allowed = capped(
                query_norm, key_block, query_docs, key_docs, query_pos, key_pos
            )
            prob_block = jnp.where(allowed, jnp.exp(scores - log_total[..., None]), 0.0)
            dprob = jnp.einsum(
                "qhge,khe->hgqk", gradient_rows, value_block, preferred_element_type=jnp.float32
            )
            dscore = (
                prob_block * (dprob - row_inner[..., None]) * (1.0 - (scores / CAP_VALUE) ** 2)
            ).astype(jnp.bfloat16)
            prob_low = prob_block.astype(jnp.bfloat16)
            query_part = jnp.einsum(
                "hgqk,khe->qhge", dscore, key_block, preferred_element_type=jnp.float32
            )
            key_part = jnp.einsum(
                "hgqk,qhge->khe", dscore, query_norm, preferred_element_type=jnp.float32
            )
            value_part = jnp.einsum(
                "hgqk,qhge->khe", prob_low, gradient_rows, preferred_element_type=jnp.float32
            )
            return (query_part, key_part, value_part)

        def nothing():
            return (
                jnp.zeros((row_count, kv_heads, group_width, HEAD_WIDTH), jnp.float32),
                jnp.zeros((row_count, kv_heads, HEAD_WIDTH), jnp.float32),
                jnp.zeros((row_count, kv_heads, HEAD_WIDTH), jnp.float32),
            )

        query_part, key_part, value_part = lax.cond(needed, differentiate, nothing)
        query_total_sum = query_total_sum + query_part
        partials.append((key_part, value_part))
    key_total, value_total = partials[0]
    for offset in range(1, REACH + 1):
        arrived = passed_along(for_sending(partials[offset]), "ctx", -offset)
        key_total = key_total + arrived[0]
        value_total = value_total + arrived[1]
    query_gradient = norm_grad(
        query_entries, query_inv, query_gain, QUERY_SCALE, query_total_sum
    ).astype(jnp.bfloat16)
    key_gradient = norm_grad(key_entries, key_inv, key_gain, 1.0, key_total).astype(jnp.bfloat16)
    value_gradient = value_total.astype(jnp.bfloat16)
    leaving = jnp.concatenate(
        [
            part.reshape(row_count, -1)
            for part in (attended, query_gradient, key_gradient, value_gradient)
        ],
        axis=-1,
    )
    home = lax.all_to_all(
        leaving.reshape(row_count, 1, -1), "head", split_axis=0, concat_axis=1, tiled=True
    )
    return (
        home[:, :, : cuts[0]].reshape(token_rows, -1),
        home[:, :, cuts[0] : 2 * cuts[0]].reshape(token_rows, -1),
        home[:, :, 2 * cuts[0] : 2 * cuts[0] + widths[1]].reshape(token_rows, -1),
        home[:, :, 2 * cuts[0] + widths[1] :].reshape(token_rows, -1),
    )


def solution(mesh):
    placed = (
        P(("ctx", "head"), None),
        P(("ctx", "head"), None),
        P(("ctx", "head"), None),
        P(("ctx", "head"), None),
        P(),
        P(),
        P(),
    )
    return jax.shard_map(
        on_device,
        mesh=mesh,
        in_specs=placed,
        out_specs=(
            P(("ctx", "head"), None),
            P(("ctx", "head"), None),
            P(("ctx", "head"), None),
            P(("ctx", "head"), None),
        ),
        check_vma=False,
    )
```

```python
import jax
import jax.numpy as jnp
from jax import lax
from jax.sharding import PartitionSpec as P

HEAD_WIDTH = 128
REACH = 2


CAP_VALUE = 50.0
QUERY_SCALE = 144.0 ** (-0.5)
EPSILON = 1e-06


def passed_along(block, axis, distance):
    devices = range(lax.axis_size(axis))
    route = [(i - distance, i) for i in devices if i - distance in devices]
    return lax.ppermute(block, axis, route)


def for_sending(value):

    def short(part):
        return part.astype(jnp.bfloat16) if part.dtype == jnp.float32 else part

    return jax.tree.map(short, value)


def normalize(value_entries, gain_vector, factor):
    inverse = lax.rsqrt(jnp.mean(value_entries * value_entries, axis=-1, keepdims=True) + EPSILON)
    return (inverse, (value_entries * inverse * gain_vector * factor).astype(jnp.bfloat16))


def norm_grad(value_entries, inverse, gain_vector, factor, upstream):
    scaled = upstream * gain_vector * factor
    inner_mean = jnp.mean(scaled * value_entries, axis=-1, keepdims=True)
    return inverse * (scaled - value_entries * inverse * inverse * inner_mean)


def capped(query_block, key_block, query_docs, key_docs, query_pos, key_pos):
    raw_scores = jnp.einsum(
        "qhge,khe->hgqk", query_block, key_block, preferred_element_type=jnp.float32
    )
    scores = CAP_VALUE * jnp.tanh(raw_scores / CAP_VALUE)
    allowed = (query_docs[:, None] == key_docs[None, :]) & (key_pos[None, :] <= query_pos[:, None])
    return (scores, allowed)


def on_device(
    query_matrix, key_matrix, value_matrix, output_gradient, query_gain, key_gain, doc_ids
):
    token_rows, head_devices = query_matrix.shape[0], lax.axis_size("head")
    packed = jnp.concatenate(
        [
            part.reshape(token_rows, head_devices, -1)
            for part in (query_matrix, key_matrix, value_matrix, output_gradient)
        ],
        axis=-1,
    )
    arrived = lax.all_to_all(packed, "head", split_axis=1, concat_axis=0, tiled=True)
    arrived = arrived.reshape(token_rows * head_devices, -1)
    widths = [query_matrix.shape[1] // head_devices, key_matrix.shape[1] // head_devices]
    cuts = [widths[0], widths[0] + widths[1], widths[0] + 2 * widths[1]]
    query_loc = arrived[:, : cuts[0]]
    key_loc = arrived[:, cuts[0] : cuts[1]]
    value_loc = arrived[:, cuts[1] : cuts[2]]
    grad_loc = arrived[:, cuts[2] :]
    row_count = query_loc.shape[0]
    kv_heads = key_loc.shape[1] // HEAD_WIDTH
    group_width = query_loc.shape[1] // key_loc.shape[1]
    query_entries = query_loc.astype(jnp.float32).reshape(
        row_count, kv_heads, group_width, HEAD_WIDTH
    )
    key_entries = key_loc.astype(jnp.float32).reshape(row_count, kv_heads, HEAD_WIDTH)
    query_inv, query_norm = normalize(query_entries, query_gain, QUERY_SCALE)
    key_inv, key_norm_factor = normalize(key_entries, key_gain, 1.0)
    value_entries = value_loc.reshape(row_count, kv_heads, HEAD_WIDTH)
    gradient_rows = grad_loc.reshape(row_count, kv_heads, group_width, HEAD_WIDTH)
    ctx_place = lax.axis_index("ctx")
    row_start = ctx_place * row_count
    query_docs = lax.dynamic_slice_in_dim(doc_ids, row_start, row_count, 0)
    query_pos = row_start + jnp.arange(row_count, dtype=jnp.int32)
    own_pair = jnp.concatenate([key_norm_factor, value_entries], axis=-1)
    pairs = [own_pair] + [
        passed_along(own_pair, "ctx", offset) for offset in range(1, REACH + 1)
    ]
    window = jnp.concatenate(pairs[::-1], axis=0)
    key_window = window[..., :HEAD_WIDTH]
    value_window = window[..., HEAD_WIDTH:]
    window_rows = (REACH + 1) * row_count
    key_pos = row_start - REACH * row_count + jnp.arange(window_rows, dtype=jnp.int32)
    padded_docs = jnp.concatenate(
        [jnp.full((REACH * row_count,), -1, jnp.int32), doc_ids.astype(jnp.int32)]
    )
    key_docs = lax.dynamic_slice_in_dim(padded_docs, row_start, window_rows, 0)
    scores, allowed = capped(query_norm, key_window, query_docs, key_docs, query_pos, key_pos)
    weights = jnp.where(allowed, jnp.exp(scores), 0.0)
    weight_sum = jnp.sum(weights, axis=-1)
    mixed_sum = jnp.einsum(
        "hgqk,khe->qhge",
        weights.astype(jnp.bfloat16),
        value_window,
        preferred_element_type=jnp.float32,
    )
    attended = (mixed_sum / jnp.transpose(weight_sum, (2, 0, 1))[..., None]).astype(jnp.bfloat16)
    log_total = jnp.log(weight_sum)
    row_inner = jnp.transpose(
        jnp.sum(gradient_rows.astype(jnp.float32) * attended.astype(jnp.float32), axis=-1),
        (1, 2, 0),
    )
    prob_block = jnp.where(allowed, jnp.exp(scores - log_total[..., None]), 0.0)
    dprob = jnp.einsum(
        "qhge,khe->hgqk", gradient_rows, value_window, preferred_element_type=jnp.float32
    )
    dscore = (
        prob_block * (dprob - row_inner[..., None]) * (1.0 - (scores / CAP_VALUE) ** 2)
    ).astype(jnp.bfloat16)
    prob_low = prob_block.astype(jnp.bfloat16)
    query_total_sum = jnp.einsum(
        "hgqk,khe->qhge", dscore, key_window, preferred_element_type=jnp.float32
    )
    key_part = jnp.einsum(
        "hgqk,qhge->khe", dscore, query_norm, preferred_element_type=jnp.float32
    )
    value_part = jnp.einsum(
        "hgqk,qhge->khe", prob_low, gradient_rows, preferred_element_type=jnp.float32
    )
    key_total = key_part[REACH * row_count :]
    value_total = value_part[REACH * row_count :]
    grad_parts = jnp.concatenate([key_part, value_part], axis=-1)
    for offset in range(1, REACH + 1):
        first = (REACH - offset) * row_count
        arrived = passed_along(
            for_sending(grad_parts[first : first + row_count]), "ctx", -offset
        )
        key_total = key_total + arrived[..., :HEAD_WIDTH]
        value_total = value_total + arrived[..., HEAD_WIDTH:]
    query_gradient = norm_grad(
        query_entries, query_inv, query_gain, QUERY_SCALE, query_total_sum
    ).astype(jnp.bfloat16)
    key_gradient = norm_grad(key_entries, key_inv, key_gain, 1.0, key_total).astype(jnp.bfloat16)
    value_gradient = value_total.astype(jnp.bfloat16)
    leaving = jnp.concatenate(
        [
            part.reshape(row_count, -1)
            for part in (attended, query_gradient, key_gradient, value_gradient)
        ],
        axis=-1,
    )
    home = lax.all_to_all(
        leaving.reshape(row_count, 1, -1), "head", split_axis=0, concat_axis=1, tiled=True
    )
    return (
        home[:, :, : cuts[0]].reshape(token_rows, -1),
        home[:, :, cuts[0] : 2 * cuts[0]].reshape(token_rows, -1),
        home[:, :, 2 * cuts[0] : 2 * cuts[0] + widths[1]].reshape(token_rows, -1),
        home[:, :, 2 * cuts[0] + widths[1] :].reshape(token_rows, -1),
    )


def solution(mesh):
    placed = (
        P(("ctx", "head"), None),
        P(("ctx", "head"), None),
        P(("ctx", "head"), None),
        P(("ctx", "head"), None),
        P(),
        P(),
        P(),
    )
    return jax.shard_map(
        on_device,
        mesh=mesh,
        in_specs=placed,
        out_specs=(
            P(("ctx", "head"), None),
            P(("ctx", "head"), None),
            P(("ctx", "head"), None),
            P(("ctx", "head"), None),
        ),
        check_vma=False,
    )
```

```python
import jax
import jax.numpy as jnp
from jax import lax
from jax.sharding import PartitionSpec as P

HEAD_WIDTH = 128
REACH = 2
Z_PARTS = 4


CAP_VALUE = 50.0
QUERY_SCALE = 144.0 ** (-0.5)
EPSILON = 1e-06


def passed_along(block, axis, distance):
    devices = range(lax.axis_size(axis))
    route = [(i - distance, i) for i in devices if i - distance in devices]
    return lax.ppermute(block, axis, route)


def for_sending(value):

    def short(part):
        return part.astype(jnp.bfloat16) if part.dtype == jnp.float32 else part

    return jax.tree.map(short, value)


def head_place():
    me = lax.axis_index("head")
    return me // Z_PARTS, me % Z_PARTS


def shifted(block, step, along):
    size = lax.axis_size("head")
    x_parts = size // Z_PARTS

    def target(i):
        hx, hz = divmod(i, Z_PARTS)
        if along == "z":
            return hx * Z_PARTS + (hz + step) % Z_PARTS
        return ((hx + step) % x_parts) * Z_PARTS + hz

    return lax.ppermute(block, "head", [(i, target(i)) for i in range(size)])


def mirrored(block, hx, hz):
    block = jnp.roll(jnp.flip(block, 0), hx + 1, 0)
    return jnp.roll(jnp.flip(block, 1), hz + 1, 1)


def to_heads(block):
    x_parts, z_parts = block.shape[1], block.shape[2]
    hx, hz = head_place()
    got = []
    for k in range(z_parts):
        piece = lax.dynamic_index_in_dim(block, (hz + k) % z_parts, 2, keepdims=False)
        got.append(piece if k == 0 else shifted(piece, k, "z"))
    stage = jnp.stack(got, 0)
    got = []
    for k in range(x_parts):
        piece = lax.dynamic_index_in_dim(stage, (hx + k) % x_parts, 2, keepdims=False)
        got.append(piece if k == 0 else shifted(piece, k, "x"))
    ordered = mirrored(jnp.stack(got, 0), hx, hz)
    return ordered.reshape(x_parts * z_parts * block.shape[0], block.shape[-1])


def from_heads(rows, token_rows):
    x_parts = lax.axis_size("head") // Z_PARTS
    hx, hz = head_place()
    block = mirrored(rows.reshape(x_parts, Z_PARTS, token_rows, -1), hx, hz)
    back = jnp.stack(
        [block[0]] + [shifted(block[k], x_parts - k, "x") for k in range(1, x_parts)], 0
    )
    home = jnp.stack(
        [back[:, 0]]
        + [shifted(back[:, k], Z_PARTS - k, "z") for k in range(1, Z_PARTS)],
        1,
    )
    home = jnp.roll(jnp.roll(home, hx, 0), hz, 1)
    return jnp.transpose(home, (2, 0, 1, 3)).reshape(token_rows, x_parts * Z_PARTS, -1)


def normalize(value_entries, gain_vector, factor):
    inverse = lax.rsqrt(jnp.mean(value_entries * value_entries, axis=-1, keepdims=True) + EPSILON)
    return (inverse, (value_entries * inverse * gain_vector * factor).astype(jnp.bfloat16))


def norm_grad(value_entries, inverse, gain_vector, factor, upstream):
    scaled = upstream * gain_vector * factor
    inner_mean = jnp.mean(scaled * value_entries, axis=-1, keepdims=True)
    return inverse * (scaled - value_entries * inverse * inverse * inner_mean)


def one_head(query_loc, grad_loc, query_gain, key_window, value_window, allowed):
    query_entries = query_loc.astype(jnp.float32)
    query_inv, query_norm = normalize(query_entries, query_gain, QUERY_SCALE)
    raw_scores = jnp.einsum(
        "qe,ke->qk", query_norm, key_window, preferred_element_type=jnp.float32
    )
    scores = CAP_VALUE * jnp.tanh(raw_scores / CAP_VALUE)
    weights = jnp.where(allowed, jnp.exp(scores), 0.0)
    weight_sum = jnp.sum(weights, axis=-1, keepdims=True)
    mixed_sum = jnp.einsum(
        "qk,ke->qe", weights.astype(jnp.bfloat16), value_window, preferred_element_type=jnp.float32
    )
    attended = (mixed_sum / weight_sum).astype(jnp.bfloat16)
    log_total = jnp.log(weight_sum)
    row_inner = jnp.sum(
        grad_loc.astype(jnp.float32) * attended.astype(jnp.float32), axis=-1, keepdims=True
    )
    prob_block = jnp.where(allowed, jnp.exp(scores - log_total), 0.0)
    dprob = jnp.einsum("qe,ke->qk", grad_loc, value_window, preferred_element_type=jnp.float32)
    dscore = (prob_block * (dprob - row_inner) * (1.0 - (scores / CAP_VALUE) ** 2)).astype(
        jnp.bfloat16
    )
    prob_low = prob_block.astype(jnp.bfloat16)
    query_total_sum = jnp.einsum(
        "qk,ke->qe", dscore, key_window, preferred_element_type=jnp.float32
    )
    key_part = jnp.einsum("qk,qe->ke", dscore, query_norm, preferred_element_type=jnp.float32)
    value_part = jnp.einsum("qk,qe->ke", prob_low, grad_loc, preferred_element_type=jnp.float32)
    query_gradient = norm_grad(
        query_entries, query_inv, query_gain, QUERY_SCALE, query_total_sum
    ).astype(jnp.bfloat16)
    return attended, query_gradient, key_part, value_part


def on_device(
    query_matrix, key_matrix, value_matrix, output_gradient, query_gain, key_gain, doc_ids
):
    token_rows, head_devices = query_matrix.shape[0], lax.axis_size("head")
    x_parts = head_devices // Z_PARTS
    group_width = query_matrix.shape[1] // key_matrix.shape[1]
    queries = query_matrix.reshape(token_rows, head_devices, group_width, HEAD_WIDTH)
    grads = output_gradient.reshape(token_rows, head_devices, group_width, HEAD_WIDTH)
    keys = key_matrix.reshape(token_rows, head_devices, HEAD_WIDTH)
    values = value_matrix.reshape(token_rows, head_devices, HEAD_WIDTH)

    def sent(parts):
        packed = jnp.concatenate(parts, axis=-1)
        return to_heads(packed.reshape(token_rows, x_parts, Z_PARTS, -1))

    first = sent([keys, values, queries[:, :, 0], grads[:, :, 0]])
    later = [
        sent([queries[:, :, g], grads[:, :, g]]) for g in range(1, group_width)
    ]
    row_count = first.shape[0]
    key_entries = first[:, :HEAD_WIDTH].astype(jnp.float32)
    key_inv, key_norm_factor = normalize(key_entries, key_gain, 1.0)
    own_pair = jnp.concatenate([key_norm_factor, first[:, HEAD_WIDTH : 2 * HEAD_WIDTH]], axis=-1)
    pairs = [own_pair] + [
        passed_along(own_pair, "ctx", offset) for offset in range(1, REACH + 1)
    ]
    window = jnp.concatenate(pairs[::-1], axis=0)
    key_window = window[:, :HEAD_WIDTH]
    value_window = window[:, HEAD_WIDTH:]
    ctx_place = lax.axis_index("ctx")
    row_start = ctx_place * row_count
    window_rows = (REACH + 1) * row_count
    query_docs = lax.dynamic_slice_in_dim(doc_ids, row_start, row_count, 0)
    query_pos = row_start + jnp.arange(row_count, dtype=jnp.int32)
    key_pos = row_start - REACH * row_count + jnp.arange(window_rows, dtype=jnp.int32)
    padded_docs = jnp.concatenate(
        [jnp.full((REACH * row_count,), -1, jnp.int32), doc_ids.astype(jnp.int32)]
    )
    key_docs = lax.dynamic_slice_in_dim(padded_docs, row_start, window_rows, 0)
    allowed = (query_docs[:, None] == key_docs[None, :]) & (key_pos[None, :] <= query_pos[:, None])
    sources = [first[:, 2 * HEAD_WIDTH :]] + later
    results = []
    key_total = None
    for g in range(group_width):
        attended, query_gradient, key_part, value_part = one_head(
            sources[g][:, :HEAD_WIDTH],
            sources[g][:, HEAD_WIDTH:],
            query_gain,
            key_window,
            value_window,
            allowed,
        )
        if g + 1 < group_width:
            results.append(from_heads(jnp.concatenate([attended, query_gradient], -1), token_rows))
        else:
            results.append((attended, query_gradient))
        grad_parts = jnp.concatenate([key_part, value_part], axis=-1)
        key_total = grad_parts if key_total is None else key_total + grad_parts
    total = key_total[REACH * row_count :]
    for offset in range(1, REACH + 1):
        start = (REACH - offset) * row_count
        arrived = passed_along(for_sending(key_total[start : start + row_count]), "ctx", -offset)
        total = total + arrived
    key_gradient = norm_grad(
        key_entries, key_inv, key_gain, 1.0, total[:, :HEAD_WIDTH]
    ).astype(jnp.bfloat16)
    value_gradient = total[:, HEAD_WIDTH:].astype(jnp.bfloat16)
    attended, query_gradient = results[-1]
    final = from_heads(
        jnp.concatenate([attended, query_gradient, key_gradient, value_gradient], -1), token_rows
    )
    attended_heads = [r[..., :HEAD_WIDTH] for r in results[:-1]] + [final[..., :HEAD_WIDTH]]
    query_heads = [r[..., HEAD_WIDTH:] for r in results[:-1]] + [
        final[..., HEAD_WIDTH : 2 * HEAD_WIDTH]
    ]
    return (
        jnp.stack(attended_heads, 2).reshape(token_rows, -1),
        jnp.stack(query_heads, 2).reshape(token_rows, -1),
        final[..., 2 * HEAD_WIDTH : 3 * HEAD_WIDTH].reshape(token_rows, -1),
        final[..., 3 * HEAD_WIDTH :].reshape(token_rows, -1),
    )


def solution(mesh):
    placed = (
        P(("ctx", "head"), None),
        P(("ctx", "head"), None),
        P(("ctx", "head"), None),
        P(("ctx", "head"), None),
        P(),
        P(),
        P(),
    )
    return jax.shard_map(
        on_device,
        mesh=mesh,
        in_specs=placed,
        out_specs=(
            P(("ctx", "head"), None),
            P(("ctx", "head"), None),
            P(("ctx", "head"), None),
            P(("ctx", "head"), None),
        ),
        check_vma=False,
    )
```

```python
import jax
import jax.numpy as jnp
from jax import lax
from jax.sharding import PartitionSpec as P

HEAD_WIDTH = 128
REACH = 2


CAP_VALUE = 50.0
QUERY_SCALE = 144.0 ** (-0.5)
EPSILON = 1e-06


def passed_along(block, axis, distance):
    devices = range(lax.axis_size(axis))
    route = [(i - distance, i) for i in devices if i - distance in devices]
    return lax.ppermute(block, axis, route)


def for_sending(value):

    def short(part):
        return part.astype(jnp.bfloat16) if part.dtype == jnp.float32 else part

    return jax.tree.map(short, value)


def normalize(value_entries, gain_vector, factor):
    inverse = lax.rsqrt(jnp.mean(value_entries * value_entries, axis=-1, keepdims=True) + EPSILON)
    return (inverse, (value_entries * inverse * gain_vector * factor).astype(jnp.bfloat16))


def norm_grad(value_entries, inverse, gain_vector, factor, upstream):
    scaled = upstream * gain_vector * factor
    inner_mean = jnp.mean(scaled * value_entries, axis=-1, keepdims=True)
    return inverse * (scaled - value_entries * inverse * inverse * inner_mean)


def capped(query_block, key_block, query_docs, key_docs, query_pos, key_pos):
    raw_scores = jnp.einsum(
        "qhge,khe->hgqk", query_block, key_block, preferred_element_type=jnp.float32
    )
    scores = CAP_VALUE * jnp.tanh(raw_scores / CAP_VALUE)
    allowed = (query_docs[:, None] == key_docs[None, :]) & (key_pos[None, :] <= query_pos[:, None])
    return (scores, allowed)


def on_device(
    query_matrix, key_matrix, value_matrix, output_gradient, query_gain, key_gain, doc_ids
):
    token_rows, head_devices = query_matrix.shape[0], lax.axis_size("head")
    packed = jnp.concatenate(
        [
            part.reshape(token_rows, head_devices, -1)
            for part in (query_matrix, key_matrix, value_matrix, output_gradient)
        ],
        axis=-1,
    )
    arrived = lax.all_to_all(packed, "head", split_axis=1, concat_axis=0, tiled=True)
    arrived = arrived.reshape(token_rows * head_devices, -1)
    widths = [query_matrix.shape[1] // head_devices, key_matrix.shape[1] // head_devices]
    cuts = [widths[0], widths[0] + widths[1], widths[0] + 2 * widths[1]]
    query_loc = arrived[:, : cuts[0]]
    key_loc = arrived[:, cuts[0] : cuts[1]]
    value_loc = arrived[:, cuts[1] : cuts[2]]
    grad_loc = arrived[:, cuts[2] :]
    row_count = query_loc.shape[0]
    kv_heads = key_loc.shape[1] // HEAD_WIDTH
    group_width = query_loc.shape[1] // key_loc.shape[1]
    query_entries = query_loc.astype(jnp.float32).reshape(
        row_count, kv_heads, group_width, HEAD_WIDTH
    )
    key_entries = key_loc.astype(jnp.float32).reshape(row_count, kv_heads, HEAD_WIDTH)
    query_inv, query_norm = normalize(query_entries, query_gain, QUERY_SCALE)
    key_inv, key_norm_factor = normalize(key_entries, key_gain, 1.0)
    value_entries = value_loc.reshape(row_count, kv_heads, HEAD_WIDTH)
    gradient_rows = grad_loc.reshape(row_count, kv_heads, group_width, HEAD_WIDTH)
    ctx_place = lax.axis_index("ctx")
    row_start = ctx_place * row_count
    query_docs = lax.dynamic_slice_in_dim(doc_ids, row_start, row_count, 0)
    query_pos = row_start + jnp.arange(row_count, dtype=jnp.int32)
    own_pair = jnp.concatenate([key_norm_factor, value_entries], axis=-1)
    pairs = [own_pair] + [
        passed_along(own_pair, "ctx", offset) for offset in range(1, REACH + 1)
    ]
    window = jnp.concatenate(pairs[::-1], axis=0)
    key_window = window[..., :HEAD_WIDTH]
    value_window = window[..., HEAD_WIDTH:]
    window_rows = (REACH + 1) * row_count
    key_pos = row_start - REACH * row_count + jnp.arange(window_rows, dtype=jnp.int32)
    padded_docs = jnp.concatenate(
        [jnp.full((REACH * row_count,), -1, jnp.int32), doc_ids.astype(jnp.int32)]
    )
    key_docs = lax.dynamic_slice_in_dim(padded_docs, row_start, window_rows, 0)
    scores, allowed = capped(query_norm, key_window, query_docs, key_docs, query_pos, key_pos)
    weights = jnp.where(allowed, jnp.exp(scores), 0.0)
    weight_sum = jnp.sum(weights, axis=-1)
    mixed_sum = jnp.einsum(
        "hgqk,khe->qhge",
        weights.astype(jnp.bfloat16),
        value_window,
        preferred_element_type=jnp.float32,
    )
    attended = (mixed_sum / jnp.transpose(weight_sum, (2, 0, 1))[..., None]).astype(jnp.bfloat16)
    log_total = jnp.log(weight_sum)
    row_inner = jnp.transpose(
        jnp.sum(gradient_rows.astype(jnp.float32) * attended.astype(jnp.float32), axis=-1),
        (1, 2, 0),
    )
    prob_block = jnp.where(allowed, jnp.exp(scores - log_total[..., None]), 0.0)
    dprob = jnp.einsum(
        "qhge,khe->hgqk", gradient_rows, value_window, preferred_element_type=jnp.float32
    )
    dscore = (
        prob_block * (dprob - row_inner[..., None]) * (1.0 - (scores / CAP_VALUE) ** 2)
    ).astype(jnp.bfloat16)
    prob_low = prob_block.astype(jnp.bfloat16)
    query_total_sum = jnp.einsum(
        "hgqk,khe->qhge", dscore, key_window, preferred_element_type=jnp.float32
    )
    key_part = jnp.einsum(
        "hgqk,qhge->khe", dscore, query_norm, preferred_element_type=jnp.float32
    )
    value_part = jnp.einsum(
        "hgqk,qhge->khe", prob_low, gradient_rows, preferred_element_type=jnp.float32
    )
    key_total = key_part[REACH * row_count :]
    value_total = value_part[REACH * row_count :]
    grad_parts = jnp.concatenate([key_part, value_part], axis=-1)
    for offset in range(1, REACH + 1):
        first = (REACH - offset) * row_count
        arrived = passed_along(
            for_sending(grad_parts[first : first + row_count]), "ctx", -offset
        )
        key_total = key_total + arrived[..., :HEAD_WIDTH]
        value_total = value_total + arrived[..., HEAD_WIDTH:]
    query_gradient = norm_grad(
        query_entries, query_inv, query_gain, QUERY_SCALE, query_total_sum
    ).astype(jnp.bfloat16)
    key_gradient = norm_grad(key_entries, key_inv, key_gain, 1.0, key_total).astype(jnp.bfloat16)
    value_gradient = value_total.astype(jnp.bfloat16)
    early = lax.all_to_all(
        attended.reshape(row_count, 1, -1), "head", split_axis=0, concat_axis=1, tiled=True
    )
    leaving = jnp.concatenate(
        [part.reshape(row_count, -1) for part in (query_gradient, key_gradient, value_gradient)],
        axis=-1,
    )
    home = lax.all_to_all(
        leaving.reshape(row_count, 1, -1), "head", split_axis=0, concat_axis=1, tiled=True
    )
    return (
        early.reshape(token_rows, -1),
        home[:, :, : cuts[0]].reshape(token_rows, -1),
        home[:, :, cuts[0] : cuts[0] + widths[1]].reshape(token_rows, -1),
        home[:, :, cuts[0] + widths[1] :].reshape(token_rows, -1),
    )


def solution(mesh):
    placed = (
        P(("ctx", "head"), None),
        P(("ctx", "head"), None),
        P(("ctx", "head"), None),
        P(("ctx", "head"), None),
        P(),
        P(),
        P(),
    )
    return jax.shard_map(
        on_device,
        mesh=mesh,
        in_specs=placed,
        out_specs=(
            P(("ctx", "head"), None),
            P(("ctx", "head"), None),
            P(("ctx", "head"), None),
            P(("ctx", "head"), None),
        ),
        check_vma=False,
    )
```

```python
import jax
import jax.numpy as jnp
from jax import lax
from jax.sharding import PartitionSpec as P
from jax.experimental import pallas as pl
from jax.experimental.pallas import tpu as pltpu

HEAD_WIDTH = 128
REACH = 2


CAP_VALUE = 50.0
QUERY_SCALE = 144.0 ** (-0.5)
EPSILON = 1e-06
TILE = 128
INTERPRET = False


def attention_kernel(
    live_ref, query_ref, key_ref, value_ref, grad_ref, query_doc_ref, key_doc_ref,
    attended_ref, dquery_ref, dkey_ref, dvalue_ref,
):
    query_tiles = query_ref.shape[0] // TILE
    key_tiles = key_ref.shape[0] // TILE
    reach_rows = key_ref.shape[0] - query_ref.shape[0]
    dkey_ref[...] = jnp.zeros_like(dkey_ref)
    dvalue_ref[...] = jnp.zeros_like(dvalue_ref)
    query_iota = lax.broadcasted_iota(jnp.int32, (TILE, TILE), 0)
    key_iota = lax.broadcasted_iota(jnp.int32, (TILE, TILE), 1)

    def tile_scores(q_start, k_start, query_tile, query_docs):
        key_tile = key_ref[pl.ds(k_start, TILE), :]
        raw = lax.dot_general(
            query_tile, key_tile, (((1,), (1,)), ((), ())), preferred_element_type=jnp.float32
        )
        scores = CAP_VALUE * jnp.tanh(raw / CAP_VALUE)
        key_docs = key_doc_ref[:, pl.ds(k_start, TILE)]
        allowed = (query_docs == key_docs) & (
            k_start + key_iota <= q_start + reach_rows + query_iota
        )
        return key_tile, scores, allowed

    for head in range(query_ref.shape[1] // HEAD_WIDTH):
        columns = pl.ds(head * HEAD_WIDTH, HEAD_WIDTH)

        def query_step(i, carry):
            q_start = pl.multiple_of(i * TILE, TILE)
            query_tile = query_ref[pl.ds(q_start, TILE), columns]
            grad_tile = grad_ref[pl.ds(q_start, TILE), columns]
            query_docs = query_doc_ref[pl.ds(q_start, TILE), :]

            def forward_step(j, acc):
                k_start = pl.multiple_of(j * TILE, TILE)

                def work(acc):
                    _, scores, allowed = tile_scores(q_start, k_start, query_tile, query_docs)
                    weights = jnp.where(allowed, jnp.exp(scores), 0.0)
                    value_tile = value_ref[pl.ds(k_start, TILE), :]
                    mixed = jnp.dot(
                        weights.astype(jnp.bfloat16), value_tile, preferred_element_type=jnp.float32
                    )
                    return (acc[0] + jnp.sum(weights, axis=1, keepdims=True), acc[1] + mixed)

                return lax.cond(live_ref[i, j] > 0, work, lambda acc: acc, acc)

            weight_sum, mixed_sum = lax.fori_loop(
                0,
                key_tiles,
                forward_step,
                (jnp.zeros((TILE, 1), jnp.float32), jnp.zeros((TILE, HEAD_WIDTH), jnp.float32)),
            )
            attended = (mixed_sum / weight_sum).astype(jnp.bfloat16)
            attended_ref[pl.ds(q_start, TILE), columns] = attended
            log_total = jnp.log(weight_sum)
            row_inner = jnp.sum(
                grad_tile.astype(jnp.float32) * attended.astype(jnp.float32), axis=1, keepdims=True
            )

            def backward_step(j, dquery):
                k_start = pl.multiple_of(j * TILE, TILE)

                def work(dquery):
                    key_tile, scores, allowed = tile_scores(q_start, k_start, query_tile, query_docs)
                    value_tile = value_ref[pl.ds(k_start, TILE), :]
                    prob = jnp.where(allowed, jnp.exp(scores - log_total), 0.0)
                    dprob = lax.dot_general(
                        grad_tile, value_tile, (((1,), (1,)), ((), ())),
                        preferred_element_type=jnp.float32,
                    )
                    dscore = (
                        prob * (dprob - row_inner) * (1.0 - (scores / CAP_VALUE) ** 2)
                    ).astype(jnp.bfloat16)
                    rows = pl.ds(k_start, TILE)
                    dkey_ref[rows, :] += lax.dot_general(
                        dscore, query_tile, (((0,), (0,)), ((), ())),
                        preferred_element_type=jnp.float32,
                    )
                    dvalue_ref[rows, :] += lax.dot_general(
                        prob.astype(jnp.bfloat16), grad_tile, (((0,), (0,)), ((), ())),
                        preferred_element_type=jnp.float32,
                    )
                    return dquery + jnp.dot(dscore, key_tile, preferred_element_type=jnp.float32)

                return lax.cond(live_ref[i, j] > 0, work, lambda d: d, dquery)

            dquery = lax.fori_loop(
                0, key_tiles, backward_step, jnp.zeros((TILE, HEAD_WIDTH), jnp.float32)
            )
            dquery_ref[pl.ds(q_start, TILE), columns] = dquery
            return carry

        lax.fori_loop(0, query_tiles, query_step, 0)


def fused_attention(query_norm, key_window, value_window, grad_rows, query_docs, key_docs):
    rows, width = query_norm.shape
    window_rows = key_window.shape[0]
    query_span = query_docs.reshape(rows // TILE, TILE)
    key_span = key_docs.reshape(window_rows // TILE, TILE)
    reach_tiles = (window_rows - rows) // TILE
    tile_gap = jnp.arange(window_rows // TILE)[None, :] - jnp.arange(rows // TILE)[:, None]
    live = (
        (key_span[None, :, -1] >= query_span[:, None, 0])
        & (key_span[None, :, 0] <= query_span[:, None, -1])
        & (tile_gap <= reach_tiles)
    ).astype(jnp.int32)
    vmem = pl.BlockSpec(memory_space=pltpu.VMEM)
    return pl.pallas_call(
        attention_kernel,
        out_shape=(
            jax.ShapeDtypeStruct((rows, width), jnp.bfloat16),
            jax.ShapeDtypeStruct((rows, width), jnp.float32),
            jax.ShapeDtypeStruct((window_rows, HEAD_WIDTH), jnp.float32),
            jax.ShapeDtypeStruct((window_rows, HEAD_WIDTH), jnp.float32),
        ),
        in_specs=[pl.BlockSpec(memory_space=pltpu.SMEM)] + [vmem] * 6,
        out_specs=(vmem, vmem, vmem, vmem),
        interpret=INTERPRET,
    )(
        live,
        query_norm,
        key_window,
        value_window,
        grad_rows,
        query_docs.reshape(rows, 1),
        key_docs.reshape(1, window_rows),
    )


def passed_along(block, axis, distance):
    devices = range(lax.axis_size(axis))
    route = [(i - distance, i) for i in devices if i - distance in devices]
    return lax.ppermute(block, axis, route)


def for_sending(value):

    def short(part):
        return part.astype(jnp.bfloat16) if part.dtype == jnp.float32 else part

    return jax.tree.map(short, value)


def normalize(value_entries, gain_vector, factor):
    inverse = lax.rsqrt(jnp.mean(value_entries * value_entries, axis=-1, keepdims=True) + EPSILON)
    return (inverse, (value_entries * inverse * gain_vector * factor).astype(jnp.bfloat16))


def norm_grad(value_entries, inverse, gain_vector, factor, upstream):
    scaled = upstream * gain_vector * factor
    inner_mean = jnp.mean(scaled * value_entries, axis=-1, keepdims=True)
    return inverse * (scaled - value_entries * inverse * inverse * inner_mean)


def capped(query_block, key_block, query_docs, key_docs, query_pos, key_pos):
    raw_scores = jnp.einsum(
        "qhge,khe->hgqk", query_block, key_block, preferred_element_type=jnp.float32
    )
    scores = CAP_VALUE * jnp.tanh(raw_scores / CAP_VALUE)
    allowed = (query_docs[:, None] == key_docs[None, :]) & (key_pos[None, :] <= query_pos[:, None])
    return (scores, allowed)


def on_device(
    query_matrix, key_matrix, value_matrix, output_gradient, query_gain, key_gain, doc_ids
):
    token_rows, head_devices = query_matrix.shape[0], lax.axis_size("head")
    packed = jnp.concatenate(
        [
            part.reshape(token_rows, head_devices, -1)
            for part in (query_matrix, key_matrix, value_matrix, output_gradient)
        ],
        axis=-1,
    )
    arrived = lax.all_to_all(packed, "head", split_axis=1, concat_axis=0, tiled=True)
    arrived = arrived.reshape(token_rows * head_devices, -1)
    widths = [query_matrix.shape[1] // head_devices, key_matrix.shape[1] // head_devices]
    cuts = [widths[0], widths[0] + widths[1], widths[0] + 2 * widths[1]]
    query_loc = arrived[:, : cuts[0]]
    key_loc = arrived[:, cuts[0] : cuts[1]]
    value_loc = arrived[:, cuts[1] : cuts[2]]
    grad_loc = arrived[:, cuts[2] :]
    row_count = query_loc.shape[0]
    kv_heads = key_loc.shape[1] // HEAD_WIDTH
    group_width = query_loc.shape[1] // key_loc.shape[1]
    query_entries = query_loc.astype(jnp.float32).reshape(
        row_count, kv_heads, group_width, HEAD_WIDTH
    )
    key_entries = key_loc.astype(jnp.float32).reshape(row_count, kv_heads, HEAD_WIDTH)
    query_inv, query_norm = normalize(query_entries, query_gain, QUERY_SCALE)
    key_inv, key_norm_factor = normalize(key_entries, key_gain, 1.0)
    value_entries = value_loc.reshape(row_count, kv_heads, HEAD_WIDTH)
    gradient_rows = grad_loc.reshape(row_count, kv_heads, group_width, HEAD_WIDTH)
    ctx_place = lax.axis_index("ctx")
    row_start = ctx_place * row_count
    query_docs = lax.dynamic_slice_in_dim(doc_ids, row_start, row_count, 0)
    query_pos = row_start + jnp.arange(row_count, dtype=jnp.int32)
    own_pair = jnp.concatenate([key_norm_factor, value_entries], axis=-1)
    pairs = [own_pair] + [
        passed_along(own_pair, "ctx", offset) for offset in range(1, REACH + 1)
    ]
    window = jnp.concatenate(pairs[::-1], axis=0)
    key_window = window[..., :HEAD_WIDTH]
    value_window = window[..., HEAD_WIDTH:]
    window_rows = (REACH + 1) * row_count
    key_pos = row_start - REACH * row_count + jnp.arange(window_rows, dtype=jnp.int32)
    padded_docs = jnp.concatenate(
        [jnp.full((REACH * row_count,), -1, jnp.int32), doc_ids.astype(jnp.int32)]
    )
    key_docs = lax.dynamic_slice_in_dim(padded_docs, row_start, window_rows, 0)
    attended, dquery, key_part, value_part = fused_attention(
        query_norm.reshape(row_count, -1),
        key_window.reshape(window_rows, HEAD_WIDTH),
        value_window.reshape(window_rows, HEAD_WIDTH),
        gradient_rows.reshape(row_count, -1),
        query_docs.astype(jnp.int32),
        key_docs,
    )
    attended = attended.reshape(row_count, kv_heads, group_width, HEAD_WIDTH)
    query_total_sum = dquery.reshape(row_count, kv_heads, group_width, HEAD_WIDTH)
    key_part = key_part.reshape(window_rows, kv_heads, HEAD_WIDTH)
    value_part = value_part.reshape(window_rows, kv_heads, HEAD_WIDTH)
    key_total = key_part[REACH * row_count :]
    value_total = value_part[REACH * row_count :]
    grad_parts = jnp.concatenate([key_part, value_part], axis=-1)
    for offset in range(1, REACH + 1):
        first = (REACH - offset) * row_count
        arrived = passed_along(
            for_sending(grad_parts[first : first + row_count]), "ctx", -offset
        )
        key_total = key_total + arrived[..., :HEAD_WIDTH]
        value_total = value_total + arrived[..., HEAD_WIDTH:]
    query_gradient = norm_grad(
        query_entries, query_inv, query_gain, QUERY_SCALE, query_total_sum
    ).astype(jnp.bfloat16)
    key_gradient = norm_grad(key_entries, key_inv, key_gain, 1.0, key_total).astype(jnp.bfloat16)
    value_gradient = value_total.astype(jnp.bfloat16)
    leaving = jnp.concatenate(
        [
            part.reshape(row_count, -1)
            for part in (attended, query_gradient, key_gradient, value_gradient)
        ],
        axis=-1,
    )
    home = lax.all_to_all(
        leaving.reshape(row_count, 1, -1), "head", split_axis=0, concat_axis=1, tiled=True
    )
    return (
        home[:, :, : cuts[0]].reshape(token_rows, -1),
        home[:, :, cuts[0] : 2 * cuts[0]].reshape(token_rows, -1),
        home[:, :, 2 * cuts[0] : 2 * cuts[0] + widths[1]].reshape(token_rows, -1),
        home[:, :, 2 * cuts[0] + widths[1] :].reshape(token_rows, -1),
    )


def solution(mesh):
    placed = (
        P(("ctx", "head"), None),
        P(("ctx", "head"), None),
        P(("ctx", "head"), None),
        P(("ctx", "head"), None),
        P(),
        P(),
        P(),
    )
    return jax.shard_map(
        on_device,
        mesh=mesh,
        in_specs=placed,
        out_specs=(
            P(("ctx", "head"), None),
            P(("ctx", "head"), None),
            P(("ctx", "head"), None),
            P(("ctx", "head"), None),
        ),
        check_vma=False,
    )
```

```python
import jax
import jax.numpy as jnp
from jax import lax
from jax.sharding import PartitionSpec as P

HEAD_WIDTH = 128
REACH = 2


CAP_VALUE = 50.0
QUERY_SCALE = 144.0 ** (-0.5)
EPSILON = 1e-06


def passed_along(block, axis, distance):
    devices = range(lax.axis_size(axis))
    route = [(i - distance, i) for i in devices if i - distance in devices]
    return lax.ppermute(block, axis, route)


def for_sending(value):

    def short(part):
        return part.astype(jnp.bfloat16) if part.dtype == jnp.float32 else part

    return jax.tree.map(short, value)


def normalize(value_entries, gain_vector, factor):
    inverse = lax.rsqrt(jnp.mean(value_entries * value_entries, axis=-1, keepdims=True) + EPSILON)
    return (inverse, (value_entries * inverse * gain_vector * factor).astype(jnp.bfloat16))


def norm_grad(value_entries, inverse, gain_vector, factor, upstream):
    scaled = upstream * gain_vector * factor
    inner_mean = jnp.mean(scaled * value_entries, axis=-1, keepdims=True)
    return inverse * (scaled - value_entries * inverse * inverse * inner_mean)


def capped(query_block, key_block, query_docs, key_docs, query_pos, key_pos):
    raw_scores = jnp.einsum(
        "qhge,khe->hgqk", query_block, key_block, preferred_element_type=jnp.float32
    )
    scores = CAP_VALUE * jnp.tanh(raw_scores / CAP_VALUE)
    allowed = (query_docs[:, None] == key_docs[None, :]) & (key_pos[None, :] <= query_pos[:, None])
    return (scores, allowed)


def on_device(
    query_matrix, key_matrix, value_matrix, output_gradient, query_gain, key_gain, doc_ids
):
    token_rows, head_devices = query_matrix.shape[0], lax.axis_size("head")
    packed = jnp.concatenate(
        [
            jnp.swapaxes(part.reshape(token_rows, head_devices, -1), 0, 1)
            for part in (query_matrix, key_matrix, value_matrix, output_gradient)
        ],
        axis=-1,
    )
    arrived = lax.all_to_all(packed, "head", split_axis=0, concat_axis=0, tiled=True)
    arrived = arrived.reshape(token_rows * head_devices, -1)
    widths = [query_matrix.shape[1] // head_devices, key_matrix.shape[1] // head_devices]
    cuts = [widths[0], widths[0] + widths[1], widths[0] + 2 * widths[1]]
    query_loc = arrived[:, : cuts[0]]
    key_loc = arrived[:, cuts[0] : cuts[1]]
    value_loc = arrived[:, cuts[1] : cuts[2]]
    grad_loc = arrived[:, cuts[2] :]
    row_count = query_loc.shape[0]
    kv_heads = key_loc.shape[1] // HEAD_WIDTH
    group_width = query_loc.shape[1] // key_loc.shape[1]
    query_entries = query_loc.astype(jnp.float32).reshape(
        row_count, kv_heads, group_width, HEAD_WIDTH
    )
    key_entries = key_loc.astype(jnp.float32).reshape(row_count, kv_heads, HEAD_WIDTH)
    query_inv, query_norm = normalize(query_entries, query_gain, QUERY_SCALE)
    key_inv, key_norm_factor = normalize(key_entries, key_gain, 1.0)
    value_entries = value_loc.reshape(row_count, kv_heads, HEAD_WIDTH)
    gradient_rows = grad_loc.reshape(row_count, kv_heads, group_width, HEAD_WIDTH)
    ctx_place = lax.axis_index("ctx")
    row_start = ctx_place * row_count
    query_docs = lax.dynamic_slice_in_dim(doc_ids, row_start, row_count, 0)
    query_pos = row_start + jnp.arange(row_count, dtype=jnp.int32)
    own_pair = jnp.concatenate([key_norm_factor, value_entries], axis=-1)
    pairs = [own_pair] + [
        passed_along(own_pair, "ctx", offset) for offset in range(1, REACH + 1)
    ]
    window = jnp.concatenate(pairs[::-1], axis=0)
    key_window = window[..., :HEAD_WIDTH]
    value_window = window[..., HEAD_WIDTH:]
    window_rows = (REACH + 1) * row_count
    key_pos = row_start - REACH * row_count + jnp.arange(window_rows, dtype=jnp.int32)
    padded_docs = jnp.concatenate(
        [jnp.full((REACH * row_count,), -1, jnp.int32), doc_ids.astype(jnp.int32)]
    )
    key_docs = lax.dynamic_slice_in_dim(padded_docs, row_start, window_rows, 0)
    scores, allowed = capped(query_norm, key_window, query_docs, key_docs, query_pos, key_pos)
    weights = jnp.where(allowed, jnp.exp(scores), 0.0)
    weight_sum = jnp.sum(weights, axis=-1)
    mixed_sum = jnp.einsum(
        "hgqk,khe->qhge",
        weights.astype(jnp.bfloat16),
        value_window,
        preferred_element_type=jnp.float32,
    )
    attended = (mixed_sum / jnp.transpose(weight_sum, (2, 0, 1))[..., None]).astype(jnp.bfloat16)
    log_total = jnp.log(weight_sum)
    row_inner = jnp.transpose(
        jnp.sum(gradient_rows.astype(jnp.float32) * attended.astype(jnp.float32), axis=-1),
        (1, 2, 0),
    )
    prob_block = jnp.where(allowed, jnp.exp(scores - log_total[..., None]), 0.0)
    dprob = jnp.einsum(
        "qhge,khe->hgqk", gradient_rows, value_window, preferred_element_type=jnp.float32
    )
    dscore = (
        prob_block * (dprob - row_inner[..., None]) * (1.0 - (scores / CAP_VALUE) ** 2)
    ).astype(jnp.bfloat16)
    prob_low = prob_block.astype(jnp.bfloat16)
    query_total_sum = jnp.einsum(
        "hgqk,khe->qhge", dscore, key_window, preferred_element_type=jnp.float32
    )
    key_part = jnp.einsum(
        "hgqk,qhge->khe", dscore, query_norm, preferred_element_type=jnp.float32
    )
    value_part = jnp.einsum(
        "hgqk,qhge->khe", prob_low, gradient_rows, preferred_element_type=jnp.float32
    )
    key_total = key_part[REACH * row_count :]
    value_total = value_part[REACH * row_count :]
    grad_parts = jnp.concatenate([key_part, value_part], axis=-1)
    for offset in range(1, REACH + 1):
        first = (REACH - offset) * row_count
        arrived = passed_along(
            for_sending(grad_parts[first : first + row_count]), "ctx", -offset
        )
        key_total = key_total + arrived[..., :HEAD_WIDTH]
        value_total = value_total + arrived[..., HEAD_WIDTH:]
    query_gradient = norm_grad(
        query_entries, query_inv, query_gain, QUERY_SCALE, query_total_sum
    ).astype(jnp.bfloat16)
    key_gradient = norm_grad(key_entries, key_inv, key_gain, 1.0, key_total).astype(jnp.bfloat16)
    value_gradient = value_total.astype(jnp.bfloat16)
    leaving = jnp.concatenate(
        [
            part.reshape(row_count, -1)
            for part in (attended, query_gradient, key_gradient, value_gradient)
        ],
        axis=-1,
    )
    home = lax.all_to_all(
        leaving.reshape(head_devices, token_rows, -1), "head", split_axis=0, concat_axis=0, tiled=True
    )
    home = jnp.swapaxes(home, 0, 1)
    return (
        home[:, :, : cuts[0]].reshape(token_rows, -1),
        home[:, :, cuts[0] : 2 * cuts[0]].reshape(token_rows, -1),
        home[:, :, 2 * cuts[0] : 2 * cuts[0] + widths[1]].reshape(token_rows, -1),
        home[:, :, 2 * cuts[0] + widths[1] :].reshape(token_rows, -1),
    )


def solution(mesh):
    placed = (
        P(("ctx", "head"), None),
        P(("ctx", "head"), None),
        P(("ctx", "head"), None),
        P(("ctx", "head"), None),
        P(),
        P(),
        P(),
    )
    return jax.shard_map(
        on_device,
        mesh=mesh,
        in_specs=placed,
        out_specs=(
            P(("ctx", "head"), None),
            P(("ctx", "head"), None),
            P(("ctx", "head"), None),
            P(("ctx", "head"), None),
        ),
        check_vma=False,
    )
```

```python
import jax
import jax.numpy as jnp
from jax import lax
from jax.sharding import PartitionSpec as P

HEAD_WIDTH = 128
REACH = 2


CAP_VALUE = 50.0
QUERY_SCALE = 144.0 ** (-0.5)
EPSILON = 1e-06


def passed_along(block, axis, distance):
    devices = range(lax.axis_size(axis))
    route = [(i - distance, i) for i in devices if i - distance in devices]
    return lax.ppermute(block, axis, route)


def for_sending(value):

    def short(part):
        return part.astype(jnp.bfloat16) if part.dtype == jnp.float32 else part

    return jax.tree.map(short, value)


def normalize(value_entries, gain_vector, factor):
    inverse = lax.rsqrt(jnp.mean(value_entries * value_entries, axis=-1, keepdims=True) + EPSILON)
    return (inverse, (value_entries * inverse * gain_vector * factor).astype(jnp.bfloat16))


def norm_grad(value_entries, inverse, gain_vector, factor, upstream):
    scaled = upstream * gain_vector * factor
    inner_mean = jnp.mean(scaled * value_entries, axis=-1, keepdims=True)
    return inverse * (scaled - value_entries * inverse * inverse * inner_mean)


def capped(query_block, key_block, query_docs, key_docs, query_pos, key_pos):
    raw_scores = jnp.einsum(
        "qhge,khe->hgqk", query_block, key_block, preferred_element_type=jnp.float32
    )
    scores = CAP_VALUE * jnp.tanh(raw_scores / CAP_VALUE)
    allowed = (query_docs[:, None] == key_docs[None, :]) & (key_pos[None, :] <= query_pos[:, None])
    return (scores, allowed)


def on_device(
    query_matrix, key_matrix, value_matrix, output_gradient, query_gain, key_gain, doc_ids
):
    token_rows, head_devices = query_matrix.shape[0], lax.axis_size("head")
    packed = jnp.concatenate(
        [
            jnp.swapaxes(part.reshape(token_rows, head_devices, -1), 0, 1)
            for part in (query_matrix, key_matrix, value_matrix, output_gradient)
        ],
        axis=-1,
    )
    arrived = lax.all_to_all(packed, "head", split_axis=0, concat_axis=0, tiled=True)
    arrived = arrived.reshape(token_rows * head_devices, -1)
    widths = [query_matrix.shape[1] // head_devices, key_matrix.shape[1] // head_devices]
    cuts = [widths[0], widths[0] + widths[1], widths[0] + 2 * widths[1]]
    query_loc = arrived[:, : cuts[0]]
    key_loc = arrived[:, cuts[0] : cuts[1]]
    value_loc = arrived[:, cuts[1] : cuts[2]]
    grad_loc = arrived[:, cuts[2] :]
    row_count = query_loc.shape[0]
    kv_heads = key_loc.shape[1] // HEAD_WIDTH
    group_width = query_loc.shape[1] // key_loc.shape[1]
    query_entries = query_loc.astype(jnp.float32).reshape(
        row_count, kv_heads, group_width, HEAD_WIDTH
    )
    key_entries = key_loc.astype(jnp.float32).reshape(row_count, kv_heads, HEAD_WIDTH)
    query_inv, query_norm = normalize(query_entries, query_gain, QUERY_SCALE)
    key_inv, key_norm_factor = normalize(key_entries, key_gain, 1.0)
    value_entries = value_loc.reshape(row_count, kv_heads, HEAD_WIDTH)
    gradient_rows = grad_loc.reshape(row_count, kv_heads, group_width, HEAD_WIDTH)
    ctx_place = lax.axis_index("ctx")
    row_start = ctx_place * row_count
    query_docs = lax.dynamic_slice_in_dim(doc_ids, row_start, row_count, 0)
    query_pos = row_start + jnp.arange(row_count, dtype=jnp.int32)
    own_pair = jnp.concatenate([key_norm_factor, value_entries], axis=-1)
    pairs = [own_pair] + [
        passed_along(own_pair, "ctx", offset) for offset in range(1, REACH + 1)
    ]
    window = jnp.concatenate(pairs[::-1], axis=0)
    key_window = window[..., :HEAD_WIDTH]
    value_window = window[..., HEAD_WIDTH:]
    window_rows = (REACH + 1) * row_count
    key_pos = row_start - REACH * row_count + jnp.arange(window_rows, dtype=jnp.int32)
    padded_docs = jnp.concatenate(
        [jnp.full((REACH * row_count,), -1, jnp.int32), doc_ids.astype(jnp.int32)]
    )
    key_docs = lax.dynamic_slice_in_dim(padded_docs, row_start, window_rows, 0)
    scores, allowed = capped(query_norm, key_window, query_docs, key_docs, query_pos, key_pos)
    weights = jnp.where(allowed, jnp.exp(scores), 0.0)
    weight_sum = jnp.sum(weights, axis=-1)
    mixed_sum = jnp.einsum(
        "hgqk,khe->qhge",
        weights.astype(jnp.bfloat16),
        value_window,
        preferred_element_type=jnp.float32,
    )
    attended = (mixed_sum / jnp.transpose(weight_sum, (2, 0, 1))[..., None]).astype(jnp.bfloat16)
    log_total = jnp.log(weight_sum)
    row_inner = jnp.transpose(
        jnp.sum(gradient_rows.astype(jnp.float32) * attended.astype(jnp.float32), axis=-1),
        (1, 2, 0),
    )
    prob_block = weights / weight_sum[..., None]
    dprob = jnp.einsum(
        "qhge,khe->hgqk", gradient_rows, value_window, preferred_element_type=jnp.float32
    )
    dscore = (
        prob_block * (dprob - row_inner[..., None]) * (1.0 - (scores / CAP_VALUE) ** 2)
    ).astype(jnp.bfloat16)
    prob_low = prob_block.astype(jnp.bfloat16)
    query_total_sum = jnp.einsum(
        "hgqk,khe->qhge", dscore, key_window, preferred_element_type=jnp.float32
    )
    key_part = jnp.einsum(
        "hgqk,qhge->khe", dscore, query_norm, preferred_element_type=jnp.float32
    )
    value_part = jnp.einsum(
        "hgqk,qhge->khe", prob_low, gradient_rows, preferred_element_type=jnp.float32
    )
    key_total = key_part[REACH * row_count :]
    value_total = value_part[REACH * row_count :]
    grad_parts = jnp.concatenate([key_part, value_part], axis=-1)
    for offset in range(1, REACH + 1):
        first = (REACH - offset) * row_count
        arrived = passed_along(
            for_sending(grad_parts[first : first + row_count]), "ctx", -offset
        )
        key_total = key_total + arrived[..., :HEAD_WIDTH]
        value_total = value_total + arrived[..., HEAD_WIDTH:]
    query_gradient = norm_grad(
        query_entries, query_inv, query_gain, QUERY_SCALE, query_total_sum
    ).astype(jnp.bfloat16)
    key_gradient = norm_grad(key_entries, key_inv, key_gain, 1.0, key_total).astype(jnp.bfloat16)
    value_gradient = value_total.astype(jnp.bfloat16)
    leaving = jnp.concatenate(
        [
            part.reshape(row_count, -1)
            for part in (attended, query_gradient, key_gradient, value_gradient)
        ],
        axis=-1,
    )
    home = lax.all_to_all(
        leaving.reshape(head_devices, token_rows, -1), "head", split_axis=0, concat_axis=0, tiled=True
    )
    home = jnp.swapaxes(home, 0, 1)
    return (
        home[:, :, : cuts[0]].reshape(token_rows, -1),
        home[:, :, cuts[0] : 2 * cuts[0]].reshape(token_rows, -1),
        home[:, :, 2 * cuts[0] : 2 * cuts[0] + widths[1]].reshape(token_rows, -1),
        home[:, :, 2 * cuts[0] + widths[1] :].reshape(token_rows, -1),
    )


def solution(mesh):
    placed = (
        P(("ctx", "head"), None),
        P(("ctx", "head"), None),
        P(("ctx", "head"), None),
        P(("ctx", "head"), None),
        P(),
        P(),
        P(),
    )
    return jax.shard_map(
        on_device,
        mesh=mesh,
        in_specs=placed,
        out_specs=(
            P(("ctx", "head"), None),
            P(("ctx", "head"), None),
            P(("ctx", "head"), None),
            P(("ctx", "head"), None),
        ),
        check_vma=False,
    )
```

```python
import jax
import jax.numpy as jnp
from jax import lax
from jax.sharding import PartitionSpec as P

HEAD_WIDTH = 128
REACH = 2


CAP_VALUE = 50.0
QUERY_SCALE = 144.0 ** (-0.5)
EPSILON = 1e-06


def passed_along(block, axis, distance):
    devices = range(lax.axis_size(axis))
    route = [(i - distance, i) for i in devices if i - distance in devices]
    return lax.ppermute(block, axis, route)


def for_sending(value):

    def short(part):
        return part.astype(jnp.bfloat16) if part.dtype == jnp.float32 else part

    return jax.tree.map(short, value)


def normalize(value_entries, gain_vector, factor):
    inverse = lax.rsqrt(jnp.mean(value_entries * value_entries, axis=-1, keepdims=True) + EPSILON)
    return (inverse, (value_entries * inverse * gain_vector * factor).astype(jnp.bfloat16))


def norm_grad(value_entries, inverse, gain_vector, factor, upstream):
    scaled = upstream * gain_vector * factor
    inner_mean = jnp.mean(scaled * value_entries, axis=-1, keepdims=True)
    return inverse * (scaled - value_entries * inverse * inverse * inner_mean)


def capped(query_block, key_block, query_docs, key_docs, query_pos, key_pos):
    raw_scores = jnp.einsum(
        "qhge,khe->hgqk", query_block, key_block, preferred_element_type=jnp.float32
    )
    scores = CAP_VALUE * jnp.tanh(raw_scores / CAP_VALUE)
    allowed = (query_docs[:, None] == key_docs[None, :]) & (key_pos[None, :] <= query_pos[:, None])
    return (scores, allowed)


def on_device(
    query_matrix, key_matrix, value_matrix, output_gradient, query_gain, key_gain, doc_ids
):
    token_rows, head_devices = query_matrix.shape[0], lax.axis_size("head")
    packed = jnp.concatenate(
        [
            jnp.swapaxes(part.reshape(token_rows, head_devices, -1), 0, 1)
            for part in (query_matrix, key_matrix, value_matrix, output_gradient)
        ],
        axis=-1,
    )
    arrived = lax.all_to_all(packed, "head", split_axis=0, concat_axis=0, tiled=True)
    arrived = arrived.reshape(token_rows * head_devices, -1)
    widths = [query_matrix.shape[1] // head_devices, key_matrix.shape[1] // head_devices]
    cuts = [widths[0], widths[0] + widths[1], widths[0] + 2 * widths[1]]
    query_loc = arrived[:, : cuts[0]]
    key_loc = arrived[:, cuts[0] : cuts[1]]
    value_loc = arrived[:, cuts[1] : cuts[2]]
    grad_loc = arrived[:, cuts[2] :]
    row_count = query_loc.shape[0]
    kv_heads = key_loc.shape[1] // HEAD_WIDTH
    group_width = query_loc.shape[1] // key_loc.shape[1]
    query_entries = query_loc.astype(jnp.float32).reshape(
        row_count, kv_heads, group_width, HEAD_WIDTH
    )
    key_entries = key_loc.astype(jnp.float32).reshape(row_count, kv_heads, HEAD_WIDTH)
    query_inv, query_norm = normalize(query_entries, query_gain, QUERY_SCALE)
    key_inv, key_norm_factor = normalize(key_entries, key_gain, 1.0)
    value_entries = value_loc.reshape(row_count, kv_heads, HEAD_WIDTH)
    gradient_rows = grad_loc.reshape(row_count, kv_heads, group_width, HEAD_WIDTH)
    ctx_place = lax.axis_index("ctx")
    row_start = ctx_place * row_count
    query_docs = lax.dynamic_slice_in_dim(doc_ids, row_start, row_count, 0)
    query_pos = row_start + jnp.arange(row_count, dtype=jnp.int32)
    own_pair = jnp.concatenate([key_norm_factor, value_entries], axis=-1)
    pairs = [own_pair] + [
        passed_along(own_pair, "ctx", offset) for offset in range(1, REACH + 1)
    ]
    window = jnp.concatenate(pairs[::-1], axis=0)
    key_window = window[..., :HEAD_WIDTH]
    value_window = window[..., HEAD_WIDTH:]
    window_rows = (REACH + 1) * row_count
    key_pos = row_start - REACH * row_count + jnp.arange(window_rows, dtype=jnp.int32)
    padded_docs = jnp.concatenate(
        [jnp.full((REACH * row_count,), -1, jnp.int32), doc_ids.astype(jnp.int32)]
    )
    key_docs = lax.dynamic_slice_in_dim(padded_docs, row_start, window_rows, 0)
    scores, allowed = capped(query_norm, key_window, query_docs, key_docs, query_pos, key_pos)
    weights = jnp.where(allowed, jnp.exp(scores), 0.0)
    weight_sum = jnp.sum(weights, axis=-1)
    mixed_sum = jnp.einsum(
        "hgqk,khe->qhge",
        weights.astype(jnp.bfloat16),
        value_window,
        preferred_element_type=jnp.float32,
    )
    attended = (mixed_sum / jnp.transpose(weight_sum, (2, 0, 1))[..., None]).astype(jnp.bfloat16)
    log_total = jnp.log(weight_sum)
    row_inner = jnp.transpose(
        jnp.sum(gradient_rows.astype(jnp.float32) * attended.astype(jnp.float32), axis=-1),
        (1, 2, 0),
    )
    prob_block = jnp.where(allowed, jnp.exp(scores - log_total[..., None]), 0.0)
    dprob = jnp.einsum(
        "qhge,khe->hgqk", gradient_rows, value_window, preferred_element_type=jnp.float32
    )
    dscore = (
        prob_block * (dprob - row_inner[..., None]) * (1.0 - (scores / CAP_VALUE) ** 2)
    ).astype(jnp.bfloat16)
    prob_low = prob_block.astype(jnp.bfloat16)
    query_total_sum = jnp.einsum(
        "hgqk,khe->qhge", dscore, key_window, preferred_element_type=jnp.float32
    )
    reach_rows = REACH * row_count

    def key_side(low, high):
        key_part = jnp.einsum(
            "hgqk,qhge->khe", dscore[..., low:high], query_norm, preferred_element_type=jnp.float32
        )
        value_part = jnp.einsum(
            "hgqk,qhge->khe",
            prob_low[..., low:high],
            gradient_rows,
            preferred_element_type=jnp.float32,
        )
        return jnp.concatenate([key_part, value_part], axis=-1)

    remote_parts = key_side(0, reach_rows)
    arrivals = [
        passed_along(
            for_sending(remote_parts[(REACH - offset) * row_count : (REACH - offset + 1) * row_count]),
            "ctx",
            -offset,
        )
        for offset in range(1, REACH + 1)
    ]
    grad_total = key_side(reach_rows, window_rows)
    for arrived in arrivals:
        grad_total = grad_total + arrived
    key_total = grad_total[..., :HEAD_WIDTH]
    value_total = grad_total[..., HEAD_WIDTH:]
    query_gradient = norm_grad(
        query_entries, query_inv, query_gain, QUERY_SCALE, query_total_sum
    ).astype(jnp.bfloat16)
    key_gradient = norm_grad(key_entries, key_inv, key_gain, 1.0, key_total).astype(jnp.bfloat16)
    value_gradient = value_total.astype(jnp.bfloat16)
    leaving = jnp.concatenate(
        [
            part.reshape(row_count, -1)
            for part in (attended, query_gradient, key_gradient, value_gradient)
        ],
        axis=-1,
    )
    home = lax.all_to_all(
        leaving.reshape(head_devices, token_rows, -1), "head", split_axis=0, concat_axis=0, tiled=True
    )
    home = jnp.swapaxes(home, 0, 1)
    return (
        home[:, :, : cuts[0]].reshape(token_rows, -1),
        home[:, :, cuts[0] : 2 * cuts[0]].reshape(token_rows, -1),
        home[:, :, 2 * cuts[0] : 2 * cuts[0] + widths[1]].reshape(token_rows, -1),
        home[:, :, 2 * cuts[0] + widths[1] :].reshape(token_rows, -1),
    )


def solution(mesh):
    placed = (
        P(("ctx", "head"), None),
        P(("ctx", "head"), None),
        P(("ctx", "head"), None),
        P(("ctx", "head"), None),
        P(),
        P(),
        P(),
    )
    return jax.shard_map(
        on_device,
        mesh=mesh,
        in_specs=placed,
        out_specs=(
            P(("ctx", "head"), None),
            P(("ctx", "head"), None),
            P(("ctx", "head"), None),
            P(("ctx", "head"), None),
        ),
        check_vma=False,
    )
```

```python
import jax
import jax.numpy as jnp
from jax import lax
from jax.sharding import PartitionSpec as P

HEAD_WIDTH = 128
REACH = 2


CAP_VALUE = 50.0
QUERY_SCALE = 144.0 ** (-0.5)
EPSILON = 1e-06


def passed_along(block, axis, distance):
    devices = range(lax.axis_size(axis))
    route = [(i - distance, i) for i in devices if i - distance in devices]
    return lax.ppermute(block, axis, route)


def for_sending(value):

    def short(part):
        return part.astype(jnp.bfloat16) if part.dtype == jnp.float32 else part

    return jax.tree.map(short, value)


def normalize(value_entries, gain_vector, factor):
    inverse = lax.rsqrt(jnp.mean(value_entries * value_entries, axis=-1, keepdims=True) + EPSILON)
    return (inverse, (value_entries * inverse * gain_vector * factor).astype(jnp.bfloat16))


def norm_grad(value_entries, inverse, gain_vector, factor, upstream):
    scaled = upstream * gain_vector * factor
    inner_mean = jnp.mean(scaled * value_entries, axis=-1, keepdims=True)
    return inverse * (scaled - value_entries * inverse * inverse * inner_mean)


def capped(query_block, key_block, query_docs, key_docs, query_pos, key_pos):
    raw_scores = jnp.einsum(
        "qhge,khe->hgqk", query_block, key_block, preferred_element_type=jnp.float32
    )
    scores = CAP_VALUE * jnp.tanh(raw_scores / CAP_VALUE)
    allowed = (query_docs[:, None] == key_docs[None, :]) & (key_pos[None, :] <= query_pos[:, None])
    return (scores, allowed)


def on_device(
    query_matrix, key_matrix, value_matrix, output_gradient, query_gain, key_gain, doc_ids
):
    token_rows, head_devices = query_matrix.shape[0], lax.axis_size("head")
    packed = jnp.concatenate(
        [
            jnp.swapaxes(part.reshape(token_rows, head_devices, -1), 0, 1)
            for part in (query_matrix, key_matrix, value_matrix, output_gradient)
        ],
        axis=-1,
    )
    arrived = lax.all_to_all(packed, "head", split_axis=0, concat_axis=0, tiled=True)
    arrived = arrived.reshape(token_rows * head_devices, -1)
    widths = [query_matrix.shape[1] // head_devices, key_matrix.shape[1] // head_devices]
    cuts = [widths[0], widths[0] + widths[1], widths[0] + 2 * widths[1]]
    query_loc = arrived[:, : cuts[0]]
    key_loc = arrived[:, cuts[0] : cuts[1]]
    value_loc = arrived[:, cuts[1] : cuts[2]]
    grad_loc = arrived[:, cuts[2] :]
    row_count = query_loc.shape[0]
    kv_heads = key_loc.shape[1] // HEAD_WIDTH
    group_width = query_loc.shape[1] // key_loc.shape[1]
    query_entries = query_loc.astype(jnp.float32).reshape(
        row_count, kv_heads, group_width, HEAD_WIDTH
    )
    key_entries = key_loc.astype(jnp.float32).reshape(row_count, kv_heads, HEAD_WIDTH)
    query_inv, query_norm = normalize(query_entries, query_gain, QUERY_SCALE)
    key_inv, key_norm_factor = normalize(key_entries, key_gain, 1.0)
    value_entries = value_loc.reshape(row_count, kv_heads, HEAD_WIDTH)
    gradient_rows = grad_loc.reshape(row_count, kv_heads, group_width, HEAD_WIDTH)
    ctx_place = lax.axis_index("ctx")
    row_start = ctx_place * row_count
    query_docs = lax.dynamic_slice_in_dim(doc_ids, row_start, row_count, 0)
    query_pos = row_start + jnp.arange(row_count, dtype=jnp.int32)
    own_pair = jnp.concatenate([key_loc.reshape(row_count, kv_heads, HEAD_WIDTH), value_entries], axis=-1)
    pairs = [own_pair] + [
        passed_along(own_pair, "ctx", offset) for offset in range(1, REACH + 1)
    ]
    window = jnp.concatenate(pairs[::-1], axis=0)
    key_window = normalize(window[..., :HEAD_WIDTH].astype(jnp.float32), key_gain, 1.0)[1]
    value_window = window[..., HEAD_WIDTH:]
    window_rows = (REACH + 1) * row_count
    key_pos = row_start - REACH * row_count + jnp.arange(window_rows, dtype=jnp.int32)
    padded_docs = jnp.concatenate(
        [jnp.full((REACH * row_count,), -1, jnp.int32), doc_ids.astype(jnp.int32)]
    )
    key_docs = lax.dynamic_slice_in_dim(padded_docs, row_start, window_rows, 0)
    scores, allowed = capped(query_norm, key_window, query_docs, key_docs, query_pos, key_pos)
    weights = jnp.where(allowed, jnp.exp(scores), 0.0)
    weight_sum = jnp.sum(weights, axis=-1)
    mixed_sum = jnp.einsum(
        "hgqk,khe->qhge",
        weights.astype(jnp.bfloat16),
        value_window,
        preferred_element_type=jnp.float32,
    )
    attended = (mixed_sum / jnp.transpose(weight_sum, (2, 0, 1))[..., None]).astype(jnp.bfloat16)
    log_total = jnp.log(weight_sum)
    row_inner = jnp.transpose(
        jnp.sum(gradient_rows.astype(jnp.float32) * attended.astype(jnp.float32), axis=-1),
        (1, 2, 0),
    )
    prob_block = jnp.where(allowed, jnp.exp(scores - log_total[..., None]), 0.0)
    dprob = jnp.einsum(
        "qhge,khe->hgqk", gradient_rows, value_window, preferred_element_type=jnp.float32
    )
    dscore = (
        prob_block * (dprob - row_inner[..., None]) * (1.0 - (scores / CAP_VALUE) ** 2)
    ).astype(jnp.bfloat16)
    prob_low = prob_block.astype(jnp.bfloat16)
    query_total_sum = jnp.einsum(
        "hgqk,khe->qhge", dscore, key_window, preferred_element_type=jnp.float32
    )
    key_part = jnp.einsum(
        "hgqk,qhge->khe", dscore, query_norm, preferred_element_type=jnp.float32
    )
    value_part = jnp.einsum(
        "hgqk,qhge->khe", prob_low, gradient_rows, preferred_element_type=jnp.float32
    )
    key_total = key_part[REACH * row_count :]
    value_total = value_part[REACH * row_count :]
    grad_parts = jnp.concatenate([key_part, value_part], axis=-1)
    for offset in range(1, REACH + 1):
        first = (REACH - offset) * row_count
        arrived = passed_along(
            for_sending(grad_parts[first : first + row_count]), "ctx", -offset
        )
        key_total = key_total + arrived[..., :HEAD_WIDTH]
        value_total = value_total + arrived[..., HEAD_WIDTH:]
    query_gradient = norm_grad(
        query_entries, query_inv, query_gain, QUERY_SCALE, query_total_sum
    ).astype(jnp.bfloat16)
    key_gradient = norm_grad(key_entries, key_inv, key_gain, 1.0, key_total).astype(jnp.bfloat16)
    value_gradient = value_total.astype(jnp.bfloat16)
    leaving = jnp.concatenate(
        [
            part.reshape(row_count, -1)
            for part in (attended, query_gradient, key_gradient, value_gradient)
        ],
        axis=-1,
    )
    home = lax.all_to_all(
        leaving.reshape(head_devices, token_rows, -1), "head", split_axis=0, concat_axis=0, tiled=True
    )
    home = jnp.swapaxes(home, 0, 1)
    return (
        home[:, :, : cuts[0]].reshape(token_rows, -1),
        home[:, :, cuts[0] : 2 * cuts[0]].reshape(token_rows, -1),
        home[:, :, 2 * cuts[0] : 2 * cuts[0] + widths[1]].reshape(token_rows, -1),
        home[:, :, 2 * cuts[0] + widths[1] :].reshape(token_rows, -1),
    )


def solution(mesh):
    placed = (
        P(("ctx", "head"), None),
        P(("ctx", "head"), None),
        P(("ctx", "head"), None),
        P(("ctx", "head"), None),
        P(),
        P(),
        P(),
    )
    return jax.shard_map(
        on_device,
        mesh=mesh,
        in_specs=placed,
        out_specs=(
            P(("ctx", "head"), None),
            P(("ctx", "head"), None),
            P(("ctx", "head"), None),
            P(("ctx", "head"), None),
        ),
        check_vma=False,
    )
```

```python
import jax
import jax.numpy as jnp
from jax import lax
from jax.sharding import PartitionSpec as P

HEAD_WIDTH = 128
REACH = 2


CAP_VALUE = 50.0
QUERY_SCALE = 144.0 ** (-0.5)
EPSILON = 1e-06


def passed_along(block, axis, distance):
    devices = range(lax.axis_size(axis))
    route = [(i - distance, i) for i in devices if i - distance in devices]
    return lax.ppermute(block, axis, route)


def for_sending(value):

    def short(part):
        return part.astype(jnp.bfloat16) if part.dtype == jnp.float32 else part

    return jax.tree.map(short, value)


def normalize(value_entries, gain_vector, factor):
    inverse = lax.rsqrt(jnp.mean(value_entries * value_entries, axis=-1, keepdims=True) + EPSILON)
    return (inverse, (value_entries * inverse * gain_vector * factor).astype(jnp.bfloat16))


def norm_grad(value_entries, inverse, gain_vector, factor, upstream):
    scaled = upstream * gain_vector * factor
    inner_mean = jnp.mean(scaled * value_entries, axis=-1, keepdims=True)
    return inverse * (scaled - value_entries * inverse * inverse * inner_mean)


def capped(query_block, key_block, query_docs, key_docs, query_pos, key_pos):
    raw_scores = jnp.einsum(
        "qhge,khe->hgqk", query_block, key_block, preferred_element_type=jnp.float32
    )
    scores = CAP_VALUE * jnp.tanh(raw_scores / CAP_VALUE)
    allowed = (query_docs[:, None] == key_docs[None, :]) & (key_pos[None, :] <= query_pos[:, None])
    return (scores, allowed)


def on_device(
    query_matrix, key_matrix, value_matrix, output_gradient, query_gain, key_gain, doc_ids
):
    token_rows, head_devices = query_matrix.shape[0], lax.axis_size("head")
    packed = jnp.concatenate(
        [
            jnp.swapaxes(part.reshape(token_rows, head_devices, -1), 0, 1)
            for part in (key_matrix, value_matrix, query_matrix, output_gradient)
        ],
        axis=-1,
    )
    arrived = lax.all_to_all(packed, "head", split_axis=0, concat_axis=0, tiled=True)
    arrived = arrived.reshape(token_rows * head_devices, -1)
    widths = [query_matrix.shape[1] // head_devices, key_matrix.shape[1] // head_devices]
    cuts = [widths[0], widths[0] + widths[1], widths[0] + 2 * widths[1]]
    key_loc = arrived[:, : widths[1]]
    value_loc = arrived[:, widths[1] : 2 * widths[1]]
    query_loc = arrived[:, 2 * widths[1] : cuts[2]]
    grad_loc = arrived[:, cuts[2] :]
    row_count = query_loc.shape[0]
    kv_heads = key_loc.shape[1] // HEAD_WIDTH
    group_width = query_loc.shape[1] // key_loc.shape[1]
    query_entries = query_loc.astype(jnp.float32).reshape(
        row_count, kv_heads, group_width, HEAD_WIDTH
    )
    key_entries = key_loc.astype(jnp.float32).reshape(row_count, kv_heads, HEAD_WIDTH)
    query_inv, query_norm = normalize(query_entries, query_gain, QUERY_SCALE)
    key_inv, key_norm_factor = normalize(key_entries, key_gain, 1.0)
    value_entries = value_loc.reshape(row_count, kv_heads, HEAD_WIDTH)
    gradient_rows = grad_loc.reshape(row_count, kv_heads, group_width, HEAD_WIDTH)
    ctx_place = lax.axis_index("ctx")
    row_start = ctx_place * row_count
    query_docs = lax.dynamic_slice_in_dim(doc_ids, row_start, row_count, 0)
    query_pos = row_start + jnp.arange(row_count, dtype=jnp.int32)
    own_pair = arrived[:, : 2 * widths[1]].reshape(row_count, kv_heads, 2 * HEAD_WIDTH)
    pairs = [own_pair] + [
        passed_along(own_pair, "ctx", offset) for offset in range(1, REACH + 1)
    ]
    window = jnp.concatenate(pairs[::-1], axis=0)
    key_window = normalize(window[..., :HEAD_WIDTH].astype(jnp.float32), key_gain, 1.0)[1]
    value_window = window[..., HEAD_WIDTH:]
    window_rows = (REACH + 1) * row_count
    key_pos = row_start - REACH * row_count + jnp.arange(window_rows, dtype=jnp.int32)
    padded_docs = jnp.concatenate(
        [jnp.full((REACH * row_count,), -1, jnp.int32), doc_ids.astype(jnp.int32)]
    )
    key_docs = lax.dynamic_slice_in_dim(padded_docs, row_start, window_rows, 0)
    scores, allowed = capped(query_norm, key_window, query_docs, key_docs, query_pos, key_pos)
    weights = jnp.where(allowed, jnp.exp(scores), 0.0)
    weight_sum = jnp.sum(weights, axis=-1)
    mixed_sum = jnp.einsum(
        "hgqk,khe->qhge",
        weights.astype(jnp.bfloat16),
        value_window,
        preferred_element_type=jnp.float32,
    )
    attended = (mixed_sum / jnp.transpose(weight_sum, (2, 0, 1))[..., None]).astype(jnp.bfloat16)
    log_total = jnp.log(weight_sum)
    row_inner = jnp.transpose(
        jnp.sum(gradient_rows.astype(jnp.float32) * attended.astype(jnp.float32), axis=-1),
        (1, 2, 0),
    )
    prob_block = jnp.where(allowed, jnp.exp(scores - log_total[..., None]), 0.0)
    dprob = jnp.einsum(
        "qhge,khe->hgqk", gradient_rows, value_window, preferred_element_type=jnp.float32
    )
    dscore = (
        prob_block * (dprob - row_inner[..., None]) * (1.0 - (scores / CAP_VALUE) ** 2)
    ).astype(jnp.bfloat16)
    prob_low = prob_block.astype(jnp.bfloat16)
    query_total_sum = jnp.einsum(
        "hgqk,khe->qhge", dscore, key_window, preferred_element_type=jnp.float32
    )
    key_part = jnp.einsum(
        "hgqk,qhge->khe", dscore, query_norm, preferred_element_type=jnp.float32
    )
    value_part = jnp.einsum(
        "hgqk,qhge->khe", prob_low, gradient_rows, preferred_element_type=jnp.float32
    )
    key_total = key_part[REACH * row_count :]
    value_total = value_part[REACH * row_count :]
    grad_parts = jnp.concatenate([key_part, value_part], axis=-1)
    for offset in range(1, REACH + 1):
        first = (REACH - offset) * row_count
        arrived = passed_along(
            for_sending(grad_parts[first : first + row_count]), "ctx", -offset
        )
        key_total = key_total + arrived[..., :HEAD_WIDTH]
        value_total = value_total + arrived[..., HEAD_WIDTH:]
    query_gradient = norm_grad(
        query_entries, query_inv, query_gain, QUERY_SCALE, query_total_sum
    ).astype(jnp.bfloat16)
    key_gradient = norm_grad(key_entries, key_inv, key_gain, 1.0, key_total).astype(jnp.bfloat16)
    value_gradient = value_total.astype(jnp.bfloat16)
    leaving = jnp.concatenate(
        [
            part.reshape(row_count, -1)
            for part in (attended, query_gradient, key_gradient, value_gradient)
        ],
        axis=-1,
    )
    home = lax.all_to_all(
        leaving.reshape(head_devices, token_rows, -1), "head", split_axis=0, concat_axis=0, tiled=True
    )
    home = jnp.swapaxes(home, 0, 1)
    return (
        home[:, :, : cuts[0]].reshape(token_rows, -1),
        home[:, :, cuts[0] : 2 * cuts[0]].reshape(token_rows, -1),
        home[:, :, 2 * cuts[0] : 2 * cuts[0] + widths[1]].reshape(token_rows, -1),
        home[:, :, 2 * cuts[0] + widths[1] :].reshape(token_rows, -1),
    )


def solution(mesh):
    placed = (
        P(("ctx", "head"), None),
        P(("ctx", "head"), None),
        P(("ctx", "head"), None),
        P(("ctx", "head"), None),
        P(),
        P(),
        P(),
    )
    return jax.shard_map(
        on_device,
        mesh=mesh,
        in_specs=placed,
        out_specs=(
            P(("ctx", "head"), None),
            P(("ctx", "head"), None),
            P(("ctx", "head"), None),
            P(("ctx", "head"), None),
        ),
        check_vma=False,
    )
```
